512 devices in a mesh: area: 16 (over y, z_lo), tm: 32 (over z_hi, x, core).
Axes of the slice: x: 4, y: 8, z: 8 (z_hi: 4, z_lo: 2; z = z_hi * 2 + z_lo), core: 2. Of those that a mesh axis runs over, the one named last changes fastest.
Arguments:
- angle_start: bfloat16 [16, 2176, 4096], P('area', None, 'tm'), may hold values from -6 to 6
- dispatch_start: bfloat16 [16, 2176, 4096], P('area', None, 'tm'), may hold values from -6 to 6
- demand: bfloat16 [16, 2176, 4096], P('area', None, 'tm'), may hold values from -6 to 6
- price_start: bfloat16 [16, 8, 128, 4096], P('area', None, None, 'tm'), may hold values from -6 to 6
- susceptance: bfloat16 [16, 2176, 2176], P('area'), may hold values from -0.5 to 3.5
- tile_inverse: bfloat16 [16, 34, 64, 64], P('area'), may hold values from -0.1 to 0.3
- cost_slope: float32 [16, 2176], P('area'), may hold values from 0.2 to 2
- ramp_weight: float32 [16, 2176], P('area'), may hold values from 0.1 to 0.4
- partner: int32 [8, 16], replicated, may hold values from 0 to 15, as said below
- boundary: int32 [16, 8, 128], P('area'), may hold values from 0 to 2175
- tie_susceptance: float32 [16, 8, 128], P('area'), may hold values from 0.5 to 2
- tie_penalty: float32 [16, 8, 128], P('area'), may hold values from 0.2 to 1
- store_bus: int32 [16, 128], P('area'), may hold values from 0 to 2175
- store_gain: float32 [16, 128], P('area'), may hold values from 0.5 to 2
- store_output: float32 [16, 128], P('area'), may hold values from 0.5 to 1.5
- retention: float32 [16, 128, 4096], P('area', None, 'tm'), may hold values from 0.45 to 1
Outputs:
- angles: float32 [16, 2176, 4096], P('area', None, 'tm')
- dispatch: bfloat16 [16, 2176, 4096], P('area', None, 'tm')
- prices: float32 [16, 8, 128, 4096], P('area', None, None, 'tm')
- charge_state: float32 [16, 128, 4096], P('area', None, 'tm')
The draws below stay inside these ranges and needn't reach their ends.
Inputs may be any that keep to these rules, and one draw needn't show every extreme that they name: partner[r, partner[r, a]] = a and partner[r, a] != a; the 8 partners of an area are all different.
All inputs are finite; a program needn't handle non-finite values.
Results may differ from the reference program's by a relative error of at most 0.0061.
Values sent between devices are 32-bit elements; how exact they have to be, the bound alone decides.
No kernel may reach another device: no remote copies, remote signals or barrier semaphores. Data moves between devices by JAX's collectives and lax.ppermute only.
A program may use at most 128 MiB of HBM per device.

```python
import math
import jax
import jax.numpy as jnp
from jax import lax

TILE = 64
TILES = 34
BUS = 2176
TOTAL_HOURS = 4096
NETWORK_AREAS = 16
ROUNDS = 8
BND = 128
STORAGE_UNITS = 128
ITERS = 2
SWEEPS = 1


def draw_susceptance(key, part):
    key_one, key_two = jax.random.split(key, 2)
    noise_part = jnp.clip(jax.random.normal(key_one, (NETWORK_AREAS, BUS, BUS), jnp.float32), -4.0, 4.0)
    coupled = (noise_part + jnp.swapaxes(noise_part, 1, 2)) * (0.5 / math.sqrt(BUS))
    diagonal = jax.random.uniform(key_two, (NETWORK_AREAS, BUS), jnp.float32, 2.5, 3.5)
    identity = jnp.eye(BUS, dtype=jnp.float32)
    return (coupled * (1.0 - identity) + identity * diagonal[:, :, None]).astype(jnp.bfloat16)


def draw_tile_inverse(key, part):
    key_one, key_two = jax.random.split(key, 2)
    noise_part = jnp.clip(jax.random.normal(key_one, (NETWORK_AREAS, TILES, TILE, TILE), jnp.float32), -4.0, 4.0)
    coupled = noise_part * (0.09 / math.sqrt(TILE))
    diagonal = jax.random.uniform(key_two, (NETWORK_AREAS, TILES, TILE), jnp.float32, 0.2, 0.295)
    identity = jnp.eye(TILE, dtype=jnp.float32)
    return (coupled * (1.0 - identity) + identity * diagonal[:, :, :, None]).astype(jnp.bfloat16)


def draw_retention(key, part):
    random_keys = jax.random.split(key, 6)
    slow_share = 0.5
    chooser = jax.random.uniform(random_keys[0], (NETWORK_AREAS, STORAGE_UNITS), jnp.float32)
    fast_leak = jnp.exp(jax.random.uniform(random_keys[1], (NETWORK_AREAS, STORAGE_UNITS), jnp.float32, math.log(1.0 / 50.0), math.log(1.0 / 30.0)))
    slow_leak = jnp.exp(jax.random.uniform(random_keys[2], (NETWORK_AREAS, STORAGE_UNITS), jnp.float32, math.log(0.05), math.log(0.3))) / TOTAL_HOURS
    area_scale = jnp.exp(jax.random.uniform(random_keys[3], (NETWORK_AREAS, 1), jnp.float32, math.log(0.5), math.log(2.0)))
    storage_leak = jnp.where(chooser < slow_share, slow_leak, fast_leak) * area_scale
    outage_hour = jax.random.randint(random_keys[4], (NETWORK_AREAS, STORAGE_UNITS, 2), 0, TOTAL_HOURS)
    hour_numbers = jnp.arange(TOTAL_HOURS)[None, None, :]
    outage_flags = (hour_numbers == outage_hour[:, :, 0:1]) | (hour_numbers == outage_hour[:, :, 1:2])
    outage_event = jax.random.uniform(random_keys[5], (NETWORK_AREAS, STORAGE_UNITS, TOTAL_HOURS), jnp.float32, 0.5, 0.8)
    return (1.0 - storage_leak)[:, :, None] * jnp.where(outage_flags, outage_event, 1.0)


def draw_partner(key, part):
    count = NETWORK_AREAS
    key_one, key_two = jax.random.split(jax.random.fold_in(key, 7), 2)
    relabel = jax.random.permutation(key_one, count).astype(jnp.int32)
    chosen = jax.random.permutation(key_two, count - 1)[:ROUNDS].astype(jnp.int32)[:, None]
    member = jnp.arange(count).astype(jnp.int32)[None, :]
    circle = jnp.mod(2 * chosen - member, count - 1)
    base = jnp.where(member == count - 1, chosen, jnp.where(member == chosen, count - 1, circle))
    result = jnp.zeros((ROUNDS, count), jnp.int32).at[:, relabel].set(relabel[base])
    return result.astype(jnp.int32)


def with_ends(drawn, own_key, least, high):
    spot = [jax.random.randint(jax.random.fold_in(own_key, axis), (), 0, length) for axis, length in enumerate(drawn.shape)]
    main_axis = drawn.shape.index(max(drawn.shape))
    neighbour = spot[:main_axis] + [(spot[main_axis] + 1) % drawn.shape[main_axis]] + spot[main_axis + 1:]
    return drawn.at[tuple(spot)].set(least).at[tuple(neighbour)].set(high)


def block_levels(own_key, extent, cuts, low, high):
    loudness, own = 1.0, jax.random.fold_in(own_key, 6)
    for dim, parts in cuts:
        draws = jnp.exp(jax.random.uniform(jax.random.fold_in(own, dim), (parts,), jnp.float32, low / len(cuts), high / len(cuts)))
        loudness = loudness * jnp.repeat(draws, extent[dim] // parts).reshape([-1 if axis == dim else 1 for axis in range(len(extent))])
    return loudness


def noise(key, dims, width, limit, pieces=(), kind=jnp.bfloat16):
    drawn = jax.random.normal(key, dims, jnp.float32) * width
    if len(pieces) > 0:
        drawn = block_levels(key, dims, pieces, -0.22, 0.18) * drawn
    return jnp.clip(drawn, min=-limit, max=limit).astype(kind)


def setup_inputs(seed: int = 0) -> dict:
    seeds = jax.random.split(jax.random.key(seed), 17)
    return {
        "angle_start": noise(seeds[0], (NETWORK_AREAS, BUS, TOTAL_HOURS), 1.0, 6.0, ((0, 16), (2, 32))),
        "dispatch_start": noise(seeds[1], (NETWORK_AREAS, BUS, TOTAL_HOURS), 1.0, 6.0, ((0, 16), (2, 32))),
        "demand": noise(seeds[2], (NETWORK_AREAS, BUS, TOTAL_HOURS), 1.0, 6.0, ((0, 16), (2, 32))),
        "price_start": noise(seeds[3], (NETWORK_AREAS, ROUNDS, BND, TOTAL_HOURS), 1.0, 6.0, ((0, 16), (3, 32))),
        "susceptance": draw_susceptance(jax.random.fold_in(seeds[16], 71), 0),
        "tile_inverse": draw_tile_inverse(jax.random.fold_in(seeds[16], 71), 0),
        "cost_slope": jnp.clip(jnp.exp(math.log(2.0) - 2.3025851 * jax.random.uniform(seeds[6], (NETWORK_AREAS, BUS), jnp.float32) ** block_levels(seeds[6], (NETWORK_AREAS, BUS), ((0, 16),), -0.2, 0.2)), 0.2, 2.0),
        "ramp_weight": jnp.clip(0.1 + 0.3 * jax.random.uniform(seeds[7], (NETWORK_AREAS, BUS), jnp.float32) ** block_levels(seeds[7], (NETWORK_AREAS, BUS), ((0, 16),), -0.2, 0.2), 0.1, 0.4),
        "partner": draw_partner(jax.random.fold_in(seeds[16], 71), 0),
        "boundary": with_ends(jax.random.randint(seeds[9], (NETWORK_AREAS, ROUNDS, BND), 0, BUS), jax.random.fold_in(seeds[9], 1), 0, BUS - 1).astype(jnp.int32),
        "tie_susceptance": jnp.clip(jnp.exp(math.log(2.0) - 1.3862944 * jax.random.uniform(seeds[10], (NETWORK_AREAS, ROUNDS, BND), jnp.float32) ** block_levels(seeds[10], (NETWORK_AREAS, ROUNDS, BND), ((0, 16),), -0.2, 0.2)), 0.5, 2.0),
        "tie_penalty": jnp.clip(jnp.exp(math.log(1.0) - 1.609438 * jax.random.uniform(seeds[11], (NETWORK_AREAS, ROUNDS, BND), jnp.float32) ** block_levels(seeds[11], (NETWORK_AREAS, ROUNDS, BND), ((0, 16),), -0.2, 0.2)), 0.2, 1.0),
        "store_bus": with_ends(jax.random.randint(seeds[12], (NETWORK_AREAS, STORAGE_UNITS), 0, BUS), jax.random.fold_in(seeds[12], 1), 0, BUS - 1).astype(jnp.int32),
        "store_gain": jnp.clip(jnp.exp(math.log(2.0) - 1.3862944 * jax.random.uniform(seeds[13], (NETWORK_AREAS, STORAGE_UNITS), jnp.float32) ** block_levels(seeds[13], (NETWORK_AREAS, STORAGE_UNITS), ((0, 16),), -0.2, 0.2)), 0.5, 2.0),
        "store_output": jnp.clip(0.5 + 1.0 * jax.random.uniform(seeds[14], (NETWORK_AREAS, STORAGE_UNITS), jnp.float32) ** block_levels(seeds[14], (NETWORK_AREAS, STORAGE_UNITS), ((0, 16),), -0.2, 0.2), 0.5, 1.5),
        "retention": draw_retention(jax.random.fold_in(seeds[16], 71), 0),
    }


dispatch_step = 0.5

def chain_link(first_pair, second_pair):
    return (first_pair[0] * second_pair[0], second_pair[0] * first_pair[1] + second_pair[1])

def take_rows(matrix, indices):
    return matrix[indices]

def add_rows(values, indices, total_rows):
    blank = jnp.zeros((total_rows,) + values.shape[indices.ndim:], jnp.float32)
    return blank.at[indices].add(values)

def area_product(inputs):
    return jnp.dot(inputs[0], inputs[1], preferred_element_type=jnp.float32)

def reference(angle_start, dispatch_start, demand, price_start, susceptance, tile_inverse, cost_slope, ramp_weight, partner, boundary, tie_susceptance, tie_penalty, store_bus, store_gain, store_output, retention):
    angle_now = angle_start.astype(jnp.float32)
    dispatch = dispatch_start.astype(jnp.float32)
    price_now = price_start.astype(jnp.float32)
    demand_full = demand.astype(jnp.float32)
    inverse_full = tile_inverse.astype(jnp.float32)
    injection = jnp.zeros_like(angle_now)
    round_ids = jnp.arange(ROUNDS).astype(jnp.int32)[None, :]
    partner_of = partner.T
    scatter_rows = jax.vmap(add_rows, in_axes=(0, 0, None))
    charge_state = jnp.zeros_like(retention)
    for iteration in range(ITERS):
        rounded = lax.optimization_barrier(angle_now.astype(jnp.bfloat16))
        own_edge = jax.vmap(take_rows)(rounded, boundary).astype(jnp.float32)
        far_edge = own_edge[partner_of, round_ids]
        price_far = price_now[partner_of, round_ids]
        mismatch = own_edge - far_edge
        tie_flow = tie_susceptance[..., None] * mismatch + 0.5 * (price_now - price_far)
        fixed_part = demand_full - dispatch - injection + scatter_rows(tie_flow, boundary, BUS)
        balance = lax.map(area_product, (susceptance, rounded)) + fixed_part
        padded = jnp.pad(dispatch, ((0, 0), (0, 0), (1, 1)))
        bend = padded[:, :, :-2] - 2.0 * dispatch + padded[:, :, 2:]
        dispatch_next = dispatch + dispatch_step * (balance - cost_slope[:, :, None] * dispatch) + ramp_weight[:, :, None] * bend
        charge = -store_gain[:, :, None] * jax.vmap(take_rows)(balance, store_bus) / math.sqrt(TOTAL_HOURS)
        charge_state = lax.associative_scan(chain_link, (retention, charge), axis=2)[1]
        injection = scatter_rows(store_output[:, :, None] * charge_state, store_bus, BUS)
        residual = balance
        for sweep_index in range(SWEEPS):
            if sweep_index > 0:
                residual = lax.map(area_product, (susceptance, angle_now.astype(jnp.bfloat16))) + fixed_part
            sweep_rows = lax.optimization_barrier(residual.astype(jnp.bfloat16)).astype(jnp.float32)
            sweep_rows = sweep_rows.reshape(NETWORK_AREAS, TILES, TILE, TOTAL_HOURS)
            correction = jnp.einsum('atij,atjh->atih', inverse_full, sweep_rows)
            angle_now = angle_now - correction.reshape(NETWORK_AREAS, BUS, TOTAL_HOURS)
        price_now = price_now + tie_penalty[..., None] * mismatch
        dispatch = dispatch_next
    return (angle_now, dispatch.astype(jnp.bfloat16), price_now, charge_state)
```

```python
import math

import jax
import jax.numpy as jnp
from jax import lax
from jax.experimental import pallas as pl
from jax.experimental.pallas import tpu as pltpu
from jax.sharding import PartitionSpec as P

ITERS = 2


dispatch_step = 0.5


def padded_2(x, sides, width):
    for axis, dim in sides:
        size, length = (lax.axis_size(axis), x.shape[dim])
        up = [(i, (i + 1) % size) for i in range(size - 1)]
        down = [(j, i) for i, j in up]
        last = lax.slice_in_dim(x, length - width, length, axis=dim)
        leading = lax.slice_in_dim(x, 0, width, axis=dim)
        before = lax.ppermute(last, axis, up)
        after = lax.ppermute(leading, axis, down)
        x = jnp.concatenate([before, x, after], axis=dim)
    return x


def shifted_in(x, lane, step, fill):
    count = x.shape[1]
    ahead = pltpu.roll(x, step, 1)
    behind = pltpu.roll(x, count - step, 1)
    source = pltpu.roll(lane, step, 1)
    moved = jnp.where(source == lane - step, ahead, behind)
    return jnp.where(lane >= step, moved, fill)


def scan_kernel(kept_ref, charge_ref, total_ref, state_ref):
    kept = kept_ref[...]
    state = charge_ref[...]
    lane = lax.broadcasted_iota(jnp.int32, kept.shape, 1)
    step = 1
    while step < kept.shape[1]:
        state = kept * shifted_in(state, lane, step, 0.0) + state
        kept = kept * shifted_in(kept, lane, step, 1.0)
        step *= 2
    total_ref[...] = kept
    state_ref[...] = state


def window_scan(kept, charge):
    shape = jax.ShapeDtypeStruct(kept.shape, jnp.float32)
    return pl.pallas_call(scan_kernel, out_shape=(shape, shape))(kept, charge)


def carried_state(kept_last, state_last, position):
    state_in = jnp.zeros_like(state_last[0])
    for window in range(state_last.shape[0]):
        folded = kept_last[window] * state_in + state_last[window]
        state_in = jnp.where(window < position, folded, state_in)
    return state_in


def local(
    angle_start,
    dispatch_start,
    demand,
    price_start,
    susceptance,
    tile_inverse,
    cost_slope,
    ramp_weight,
    partner,
    boundary,
    tie_susceptance,
    tie_penalty,
    store_bus,
    store_gain,
    store_output,
    retention,
):
    area_count = lax.axis_size("area")
    area_here = lax.axis_index("area")
    position = lax.axis_index("tm")
    partners = jnp.take(partner, area_here, axis=1)
    edge_rows = boundary[0]
    store_rows = store_bus[0]
    matrix = susceptance[0]
    inverses = tile_inverse[0]
    tile_count = inverses.shape[0]
    tile_width = inverses.shape[1]
    bus_count = matrix.shape[0]
    hour_count = retention.shape[2]
    year_hours = hour_count * lax.axis_size("tm")
    kept_local = retention[0]
    angle_now = angle_start[0].astype(jnp.float32)
    dispatch = dispatch_start[0].astype(jnp.float32)
    price_now = price_start[0].astype(jnp.float32)
    demand_local = demand[0].astype(jnp.float32)
    tie_gain = tie_susceptance[0][:, :, None]
    penalty = tie_penalty[0][:, :, None]
    slope = cost_slope[0][:, None]
    ramp_local = ramp_weight[0][:, None]
    gain_local = store_gain[0][:, None]
    output_local = store_output[0][:, None]
    injection = jnp.zeros((bus_count, hour_count), jnp.float32)
    charge_state = jnp.zeros_like(kept_local)
    rounds, lines = edge_rows.shape

    def exchanged(parts):
        flat = jnp.concatenate([part.reshape(rounds, -1) for part in parts], axis=1)
        blank = jnp.zeros((area_count, flat.shape[1]), flat.dtype)
        sent = blank.at[partners].set(flat)
        got = lax.all_to_all(sent, "area", split_axis=0, concat_axis=0, tiled=True)
        got = jnp.take(got, partners, axis=0)
        found, at = [], 0
        for part in parts:
            width = part.size // rounds
            found.append(got[:, at : at + width].reshape(part.shape))
            at += width
        return found

    kept_total = None
    kept_last = None
    price_far = None
    penalty_far = None
    mismatch = None
    for iteration in range(ITERS):
        rounded = angle_now.astype(jnp.bfloat16)
        own_edge = rounded[edge_rows].astype(jnp.float32)
        if iteration == 0:
            far_edge, price_far, penalty_far = exchanged((own_edge, price_now, tie_penalty[0]))
            penalty_far = penalty_far[:, :, None]
        else:
            (far_edge,) = exchanged((own_edge,))
            price_far = price_far - penalty_far * mismatch
        mismatch = own_edge - far_edge
        tie_flow = tie_gain * mismatch + 0.5 * (price_now - price_far)
        spread = jnp.zeros((bus_count, hour_count), jnp.float32).at[edge_rows].add(tie_flow)
        fixed_part = demand_local - dispatch - injection + spread
        balance = jnp.dot(matrix, rounded, preferred_element_type=jnp.float32) + fixed_part
        padded = padded_2(dispatch, (("tm", 1),), 1)
        bend = padded[:, :-2] - 2.0 * dispatch + padded[:, 2:]
        dispatch_next = dispatch + dispatch_step * (balance - slope * dispatch) + ramp_local * bend
        charge = -gain_local * balance[store_rows] / math.sqrt(year_hours)
        kept_total, local_state = window_scan(kept_local, charge)
        if kept_last is None:
            kept_last = lax.all_gather(kept_total[:, -1], "tm", axis=0)
        state_last = lax.all_gather(local_state[:, -1], "tm", axis=0)
        state_in = carried_state(kept_last, state_last, position)
        charge_state = local_state + kept_total * state_in[:, None]
        injection = (
            jnp.zeros((bus_count, hour_count), jnp.float32)
            .at[store_rows]
            .add(output_local * charge_state)
        )
        sweep_rows = balance.astype(jnp.bfloat16).reshape(tile_count, tile_width, hour_count)
        correction = jnp.einsum(
            "tij,tjh->tih", inverses, sweep_rows, preferred_element_type=jnp.float32
        )
        angle_now = angle_now - correction.reshape(bus_count, hour_count)
        price_now = price_now + penalty * mismatch
        dispatch = dispatch_next
    return (
        angle_now[None],
        dispatch.astype(jnp.bfloat16)[None],
        price_now[None],
        charge_state[None],
    )


def solution(mesh):
    in_specs = (
        P("area", None, "tm"),
        P("area", None, "tm"),
        P("area", None, "tm"),
        P("area", None, None, "tm"),
        P("area", None, None),
        P("area", None, None, None),
        P("area", None),
        P("area", None),
        P(),
        P("area", None, None),
        P("area", None, None),
        P("area", None, None),
        P("area", None),
        P("area", None),
        P("area", None),
        P("area", None, "tm"),
    )
    out_specs = (
        P("area", None, "tm"),
        P("area", None, "tm"),
        P("area", None, None, "tm"),
        P("area", None, "tm"),
    )
    return jax.shard_map(local, mesh=mesh, in_specs=in_specs, out_specs=out_specs, check_vma=False)
```

```python
import math

import jax
import jax.numpy as jnp
from jax import lax
from jax.experimental import pallas as pl
from jax.experimental.pallas import tpu as pltpu
from jax.sharding import PartitionSpec as P

ITERS = 2


dispatch_step = 0.5


def padded_2(x, sides, width):
    for axis, dim in sides:
        size, length = (lax.axis_size(axis), x.shape[dim])
        up = [(i, (i + 1) % size) for i in range(size - 1)]
        down = [(j, i) for i, j in up]
        last = lax.slice_in_dim(x, length - width, length, axis=dim)
        leading = lax.slice_in_dim(x, 0, width, axis=dim)
        before = lax.ppermute(last, axis, up)
        after = lax.ppermute(leading, axis, down)
        x = jnp.concatenate([before, x, after], axis=dim)
    return x


def shifted_in(x, lane, step, fill):
    count = x.shape[1]
    ahead = pltpu.roll(x, step, 1)
    behind = pltpu.roll(x, count - step, 1)
    source = pltpu.roll(lane, step, 1)
    moved = jnp.where(source == lane - step, ahead, behind)
    return jnp.where(lane >= step, moved, fill)


def scan_kernel(kept_ref, charge_ref, total_ref, state_ref):
    kept = kept_ref[...]
    state = charge_ref[...]
    lane = lax.broadcasted_iota(jnp.int32, kept.shape, 1)
    step = 1
    while step < kept.shape[1]:
        state = kept * shifted_in(state, lane, step, 0.0) + state
        kept = kept * shifted_in(kept, lane, step, 1.0)
        step *= 2
    total_ref[...] = kept
    state_ref[...] = state


def window_scan(kept, charge):
    shape = jax.ShapeDtypeStruct(kept.shape, jnp.float32)
    return pl.pallas_call(scan_kernel, out_shape=(shape, shape))(kept, charge)


def carried_state(kept_last, state_last, position):
    state_in = jnp.zeros_like(state_last[0])
    for window in range(state_last.shape[0]):
        folded = kept_last[window] * state_in + state_last[window]
        state_in = jnp.where(window < position, folded, state_in)
    return state_in


def local(
    angle_start,
    dispatch_start,
    demand,
    price_start,
    susceptance,
    tile_inverse,
    cost_slope,
    ramp_weight,
    partner,
    boundary,
    tie_susceptance,
    tie_penalty,
    store_bus,
    store_gain,
    store_output,
    retention,
):
    area_count = lax.axis_size("area")
    area_here = lax.axis_index("area")
    position = lax.axis_index("tm")
    partners = jnp.take(partner, area_here, axis=1)
    edge_rows = boundary[0]
    store_rows = store_bus[0]
    matrix = susceptance[0]
    inverses = tile_inverse[0]
    tile_count = inverses.shape[0]
    tile_width = inverses.shape[1]
    bus_count = matrix.shape[0]
    hour_count = retention.shape[2]
    year_hours = hour_count * lax.axis_size("tm")
    kept_local = retention[0]
    angle_now = angle_start[0].astype(jnp.float32)
    dispatch = dispatch_start[0].astype(jnp.float32)
    price_now = price_start[0].astype(jnp.float32)
    demand_local = demand[0].astype(jnp.float32)
    tie_gain = tie_susceptance[0][:, :, None]
    penalty = tie_penalty[0][:, :, None]
    slope = cost_slope[0][:, None]
    ramp_local = ramp_weight[0][:, None]
    gain_local = store_gain[0][:, None]
    output_local = store_output[0][:, None]
    injection = jnp.zeros((bus_count, hour_count), jnp.float32)
    charge_state = jnp.zeros_like(kept_local)
    rounds, lines = edge_rows.shape

    def exchanged(parts):
        flat = jnp.concatenate([part.reshape(rounds, -1) for part in parts], axis=1)
        blank = jnp.zeros((area_count, flat.shape[1]), flat.dtype)
        sent = blank.at[partners].set(flat)
        got = lax.all_to_all(sent, "area", split_axis=0, concat_axis=0, tiled=True)
        got = jnp.take(got, partners, axis=0)
        found, at = [], 0
        for part in parts:
            width = part.size // rounds
            found.append(got[:, at : at + width].reshape(part.shape))
            at += width
        return found

    kept_total = None
    price_far = None
    penalty_far = None
    mismatch = None
    for iteration in range(ITERS):
        rounded = angle_now.astype(jnp.bfloat16)
        own_edge = rounded[edge_rows].astype(jnp.float32)
        if iteration == 0:
            far_edge, price_far, penalty_far = exchanged((own_edge, price_now, tie_penalty[0]))
            penalty_far = penalty_far[:, :, None]
        else:
            (far_edge,) = exchanged((own_edge,))
            price_far = price_far - penalty_far * mismatch
        mismatch = own_edge - far_edge
        tie_flow = tie_gain * mismatch + 0.5 * (price_now - price_far)
        spread = jnp.zeros((bus_count, hour_count), jnp.float32).at[edge_rows].add(tie_flow)
        fixed_part = demand_local - dispatch - injection + spread
        balance = jnp.dot(matrix, rounded, preferred_element_type=jnp.float32) + fixed_part
        padded = padded_2(dispatch, (("tm", 1),), 1)
        bend = padded[:, :-2] - 2.0 * dispatch + padded[:, 2:]
        dispatch_next = dispatch + dispatch_step * (balance - slope * dispatch) + ramp_local * bend
        charge = -gain_local * balance[store_rows] / math.sqrt(year_hours)
        kept_total, local_state = window_scan(kept_local, charge)
        ends = jnp.stack([kept_total[:, -1], local_state[:, -1]])
        copies = jnp.broadcast_to(ends, (lax.axis_size("tm"),) + ends.shape)
        ends = lax.all_to_all(copies, "tm", split_axis=0, concat_axis=0, tiled=True)
        state_in = carried_state(ends[:, 0], ends[:, 1], position)
        charge_state = local_state + kept_total * state_in[:, None]
        injection = (
            jnp.zeros((bus_count, hour_count), jnp.float32)
            .at[store_rows]
            .add(output_local * charge_state)
        )
        sweep_rows = balance.astype(jnp.bfloat16).reshape(tile_count, tile_width, hour_count)
        correction = jnp.einsum(
            "tij,tjh->tih", inverses, sweep_rows, preferred_element_type=jnp.float32
        )
        angle_now = angle_now - correction.reshape(bus_count, hour_count)
        price_now = price_now + penalty * mismatch
        dispatch = dispatch_next
    return (
        angle_now[None],
        dispatch.astype(jnp.bfloat16)[None],
        price_now[None],
        charge_state[None],
    )


def solution(mesh):
    in_specs = (
        P("area", None, "tm"),
        P("area", None, "tm"),
        P("area", None, "tm"),
        P("area", None, None, "tm"),
        P("area", None, None),
        P("area", None, None, None),
        P("area", None),
        P("area", None),
        P(),
        P("area", None, None),
        P("area", None, None),
        P("area", None, None),
        P("area", None),
        P("area", None),
        P("area", None),
        P("area", None, "tm"),
    )
    out_specs = (
        P("area", None, "tm"),
        P("area", None, "tm"),
        P("area", None, None, "tm"),
        P("area", None, "tm"),
    )
    return jax.shard_map(local, mesh=mesh, in_specs=in_specs, out_specs=out_specs, check_vma=False)
```

```python
import math

import jax
import jax.numpy as jnp
from jax import lax
from jax.experimental import pallas as pl
from jax.experimental.pallas import tpu as pltpu
from jax.sharding import PartitionSpec as P

ITERS = 2


dispatch_step = 0.5


def padded_2(x, sides, width):
    for axis, dim in sides:
        size, length = (lax.axis_size(axis), x.shape[dim])
        up = [(i, (i + 1) % size) for i in range(size - 1)]
        down = [(j, i) for i, j in up]
        last = lax.slice_in_dim(x, length - width, length, axis=dim)
        leading = lax.slice_in_dim(x, 0, width, axis=dim)
        before = lax.ppermute(last, axis, up)
        after = lax.ppermute(leading, axis, down)
        x = jnp.concatenate([before, x, after], axis=dim)
    return x


def shifted_in(x, lane, step, fill):
    count = x.shape[1]
    ahead = pltpu.roll(x, step, 1)
    behind = pltpu.roll(x, count - step, 1)
    source = pltpu.roll(lane, step, 1)
    moved = jnp.where(source == lane - step, ahead, behind)
    return jnp.where(lane >= step, moved, fill)


def scan_kernel(kept_ref, charge_ref, total_ref, state_ref):
    kept = kept_ref[...]
    state = charge_ref[...]
    lane = lax.broadcasted_iota(jnp.int32, kept.shape, 1)
    step = 1
    while step < kept.shape[1]:
        state = kept * shifted_in(state, lane, step, 0.0) + state
        kept = kept * shifted_in(kept, lane, step, 1.0)
        step *= 2
    total_ref[...] = kept
    state_ref[...] = state


def window_scan(kept, charge):
    shape = jax.ShapeDtypeStruct(kept.shape, jnp.float32)
    return pl.pallas_call(scan_kernel, out_shape=(shape, shape))(kept, charge)


def carried_state(kept_last, state_last, position):
    state_in = jnp.zeros_like(state_last[0])
    for window in range(state_last.shape[0]):
        folded = kept_last[window] * state_in + state_last[window]
        state_in = jnp.where(window < position, folded, state_in)
    return state_in


def local(
    angle_start,
    dispatch_start,
    demand,
    price_start,
    susceptance,
    tile_inverse,
    cost_slope,
    ramp_weight,
    partner,
    boundary,
    tie_susceptance,
    tie_penalty,
    store_bus,
    store_gain,
    store_output,
    retention,
):
    area_count = lax.axis_size("area")
    area_here = lax.axis_index("area")
    position = lax.axis_index("tm")
    partners = jnp.take(partner, area_here, axis=1)
    edge_rows = boundary[0]
    store_rows = store_bus[0]
    matrix = susceptance[0]
    inverses = tile_inverse[0]
    tile_count = inverses.shape[0]
    tile_width = inverses.shape[1]
    bus_count = matrix.shape[0]
    hour_count = retention.shape[2]
    year_hours = hour_count * lax.axis_size("tm")
    kept_local = retention[0]
    angle_now = angle_start[0].astype(jnp.float32)
    dispatch = dispatch_start[0].astype(jnp.float32)
    price_now = price_start[0].astype(jnp.float32)
    demand_local = demand[0].astype(jnp.float32)
    tie_gain = tie_susceptance[0][:, :, None]
    penalty = tie_penalty[0][:, :, None]
    slope = cost_slope[0][:, None]
    ramp_local = ramp_weight[0][:, None]
    gain_local = store_gain[0][:, None]
    output_local = store_output[0][:, None]
    injection = jnp.zeros((bus_count, hour_count), jnp.float32)
    charge_state = jnp.zeros_like(kept_local)
    rounds, lines = edge_rows.shape

    def to_partner(flat):
        slot = lax.broadcasted_iota(jnp.int32, (area_count, 1), 0)
        sent = jnp.zeros((area_count, flat.shape[1]), flat.dtype)
        for r in range(rounds):
            sent = jnp.where(slot == partners[r], flat[r][None, :], sent)
        return sent

    def from_partner(flat, parts):
        got = lax.all_to_all(flat, "area", split_axis=0, concat_axis=0, tiled=True)
        slot = lax.broadcasted_iota(jnp.int32, (area_count, 1), 0)
        picked = jnp.stack(
            [jnp.sum(jnp.where(slot == partners[r], got, 0.0), axis=0) for r in range(rounds)]
        )
        found, at = [], 0
        for part in parts:
            width = part.size // rounds
            found.append(picked[:, at : at + width].reshape(part.shape))
            at += width
        return found

    def packed(parts):
        return to_partner(jnp.concatenate([part.reshape(rounds, -1) for part in parts], axis=1))

    bus_ids = lax.broadcasted_iota(jnp.int32, (1, bus_count), 1)
    edge_pick = (edge_rows.reshape(-1, 1) == bus_ids).astype(jnp.bfloat16)
    store_pick = (store_rows.reshape(-1, 1) == bus_ids).astype(jnp.float32)
    exact = lax.Precision.HIGHEST

    def spread_rows(pick, values):
        return lax.dot_general(
            pick, values, (((0,), (0,)), ((), ())), precision=exact,
            preferred_element_type=jnp.float32,
        )

    kept_total = None
    price_far = None
    penalty_far = None
    mismatch = None
    sent = None
    for iteration in range(ITERS):
        rounded = angle_now.astype(jnp.bfloat16)
        if iteration == 0:
            own_edge = jnp.dot(edge_pick, rounded, preferred_element_type=jnp.float32)
        else:
            own_edge = next_edge
        own_edge = own_edge.reshape(rounds, lines, hour_count)
        if iteration == 0:
            parts = (own_edge, price_now, tie_penalty[0])
            far_edge, price_far, penalty_far = from_partner(packed(parts), parts)
            penalty_far = penalty_far[:, :, None]
        else:
            far_edge, = from_partner(sent, (own_edge,))
            price_far = price_far - penalty_far * mismatch
        mismatch = own_edge - far_edge
        tie_flow = tie_gain * mismatch + 0.5 * (price_now - price_far)
        spread = spread_rows(
            edge_pick.astype(jnp.float32), tie_flow.reshape(rounds * lines, hour_count)
        )
        fixed_part = demand_local - dispatch - injection + spread
        balance = jnp.dot(matrix, rounded, preferred_element_type=jnp.float32) + fixed_part
        padded = padded_2(dispatch, (("tm", 1),), 1)
        bend = padded[:, :-2] - 2.0 * dispatch + padded[:, 2:]
        dispatch_next = dispatch + dispatch_step * (balance - slope * dispatch) + ramp_local * bend
        store_balance = jnp.dot(store_pick, balance, precision=exact, preferred_element_type=jnp.float32)
        charge = -gain_local * store_balance / math.sqrt(year_hours)
        kept_total, local_state = window_scan(kept_local, charge)
        sweep_rows = balance.astype(jnp.bfloat16).reshape(tile_count, tile_width, hour_count)
        correction = jnp.einsum(
            "tij,tjh->tih", inverses, sweep_rows, preferred_element_type=jnp.float32
        )
        angle_now = angle_now - correction.reshape(bus_count, hour_count)
        ends = jnp.stack([kept_total[:, -1], local_state[:, -1]])
        if iteration + 1 < ITERS:
            next_edge = jnp.dot(
                edge_pick, angle_now.astype(jnp.bfloat16), preferred_element_type=jnp.float32
            )
            sent = packed((next_edge,))
        copies = jnp.broadcast_to(ends, (lax.axis_size("tm"),) + ends.shape)
        ends = lax.all_to_all(copies, "tm", split_axis=0, concat_axis=0, tiled=True)
        state_in = carried_state(ends[:, 0], ends[:, 1], position)
        charge_state = local_state + kept_total * state_in[:, None]
        injection = spread_rows(store_pick, output_local * charge_state)
        price_now = price_now + penalty * mismatch
        dispatch = dispatch_next
    return (
        angle_now[None],
        dispatch.astype(jnp.bfloat16)[None],
        price_now[None],
        charge_state[None],
    )


def solution(mesh):
    in_specs = (
        P("area", None, "tm"),
        P("area", None, "tm"),
        P("area", None, "tm"),
        P("area", None, None, "tm"),
        P("area", None, None),
        P("area", None, None, None),
        P("area", None),
        P("area", None),
        P(),
        P("area", None, None),
        P("area", None, None),
        P("area", None, None),
        P("area", None),
        P("area", None),
        P("area", None),
        P("area", None, "tm"),
    )
    out_specs = (
        P("area", None, "tm"),
        P("area", None, "tm"),
        P("area", None, None, "tm"),
        P("area", None, "tm"),
    )
    return jax.shard_map(local, mesh=mesh, in_specs=in_specs, out_specs=out_specs, check_vma=False)
```

```python
import math

import jax
import jax.numpy as jnp
from jax import lax
from jax.experimental import pallas as pl
from jax.experimental.pallas import tpu as pltpu
from jax.sharding import PartitionSpec as P

ITERS = 2


dispatch_step = 0.5


def padded_2(x, sides, width):
    for axis, dim in sides:
        size, length = (lax.axis_size(axis), x.shape[dim])
        up = [(i, (i + 1) % size) for i in range(size - 1)]
        down = [(j, i) for i, j in up]
        last = lax.slice_in_dim(x, length - width, length, axis=dim)
        leading = lax.slice_in_dim(x, 0, width, axis=dim)
        before = lax.ppermute(last, axis, up)
        after = lax.ppermute(leading, axis, down)
        x = jnp.concatenate([before, x, after], axis=dim)
    return x


def shifted_in(x, lane, step, fill):
    count = x.shape[1]
    ahead = pltpu.roll(x, step, 1)
    behind = pltpu.roll(x, count - step, 1)
    source = pltpu.roll(lane, step, 1)
    moved = jnp.where(source == lane - step, ahead, behind)
    return jnp.where(lane >= step, moved, fill)


def scan_kernel(kept_ref, charge_ref, total_ref, state_ref):
    kept = kept_ref[...]
    state = charge_ref[...]
    lane = lax.broadcasted_iota(jnp.int32, kept.shape, 1)
    step = 1
    while step < kept.shape[1]:
        state = kept * shifted_in(state, lane, step, 0.0) + state
        kept = kept * shifted_in(kept, lane, step, 1.0)
        step *= 2
    total_ref[...] = kept
    state_ref[...] = state


def window_scan(kept, charge):
    shape = jax.ShapeDtypeStruct(kept.shape, jnp.float32)
    return pl.pallas_call(scan_kernel, out_shape=(shape, shape))(kept, charge)


def carried_state(kept_end, state_end, position, count):
    def passed(ends, step):
        pairs = [(i, i + step) for i in range(count - step)]
        got = lax.ppermute(ends, "tm", pairs)
        have = position >= step
        return jnp.where(have, got[0], 1.0), jnp.where(have, got[1], 0.0)

    kept, state = passed(jnp.stack([kept_end, state_end]), 1)
    step = 1
    while step < count:
        kept_before, state_before = passed(jnp.stack([kept, state]), step)
        state = kept * state_before + state
        kept = kept_before * kept
        step *= 2
    return state


def local(
    angle_start,
    dispatch_start,
    demand,
    price_start,
    susceptance,
    tile_inverse,
    cost_slope,
    ramp_weight,
    partner,
    boundary,
    tie_susceptance,
    tie_penalty,
    store_bus,
    store_gain,
    store_output,
    retention,
):
    area_count = lax.axis_size("area")
    area_here = lax.axis_index("area")
    position = lax.axis_index("tm")
    partners = jnp.take(partner, area_here, axis=1)
    edge_rows = boundary[0]
    store_rows = store_bus[0]
    matrix = susceptance[0]
    inverses = tile_inverse[0]
    tile_count = inverses.shape[0]
    tile_width = inverses.shape[1]
    bus_count = matrix.shape[0]
    hour_count = retention.shape[2]
    year_hours = hour_count * lax.axis_size("tm")
    kept_local = retention[0]
    angle_now = angle_start[0].astype(jnp.float32)
    dispatch = dispatch_start[0].astype(jnp.float32)
    price_now = price_start[0].astype(jnp.float32)
    demand_local = demand[0].astype(jnp.float32)
    tie_gain = tie_susceptance[0][:, :, None]
    penalty = tie_penalty[0][:, :, None]
    slope = cost_slope[0][:, None]
    ramp_local = ramp_weight[0][:, None]
    gain_local = store_gain[0][:, None]
    output_local = store_output[0][:, None]
    injection = jnp.zeros((bus_count, hour_count), jnp.float32)
    charge_state = jnp.zeros_like(kept_local)
    rounds, lines = edge_rows.shape

    def exchanged(parts):
        flat = jnp.concatenate([part.reshape(rounds, -1) for part in parts], axis=1)
        blank = jnp.zeros((area_count, flat.shape[1]), flat.dtype)
        sent = blank.at[partners].set(flat)
        got = lax.all_to_all(sent, "area", split_axis=0, concat_axis=0, tiled=True)
        got = jnp.take(got, partners, axis=0)
        found, at = [], 0
        for part in parts:
            width = part.size // rounds
            found.append(got[:, at : at + width].reshape(part.shape))
            at += width
        return found

    kept_total = None
    price_far = None
    penalty_far = None
    mismatch = None
    for iteration in range(ITERS):
        rounded = angle_now.astype(jnp.bfloat16)
        own_edge = rounded[edge_rows].astype(jnp.float32)
        if iteration == 0:
            far_edge, price_far, penalty_far = exchanged((own_edge, price_now, tie_penalty[0]))
            penalty_far = penalty_far[:, :, None]
        else:
            (far_edge,) = exchanged((own_edge,))
            price_far = price_far - penalty_far * mismatch
        mismatch = own_edge - far_edge
        tie_flow = tie_gain * mismatch + 0.5 * (price_now - price_far)
        spread = jnp.zeros((bus_count, hour_count), jnp.float32).at[edge_rows].add(tie_flow)
        fixed_part = demand_local - dispatch - injection + spread
        balance = jnp.dot(matrix, rounded, preferred_element_type=jnp.float32) + fixed_part
        padded = padded_2(dispatch, (("tm", 1),), 1)
        bend = padded[:, :-2] - 2.0 * dispatch + padded[:, 2:]
        dispatch_next = dispatch + dispatch_step * (balance - slope * dispatch) + ramp_local * bend
        charge = -gain_local * balance[store_rows] / math.sqrt(year_hours)
        kept_total, local_state = window_scan(kept_local, charge)
        state_in = carried_state(
            kept_total[:, -1], local_state[:, -1], position, lax.axis_size("tm")
        )
        charge_state = local_state + kept_total * state_in[:, None]
        injection = (
            jnp.zeros((bus_count, hour_count), jnp.float32)
            .at[store_rows]
            .add(output_local * charge_state)
        )
        sweep_rows = balance.astype(jnp.bfloat16).reshape(tile_count, tile_width, hour_count)
        correction = jnp.einsum(
            "tij,tjh->tih", inverses, sweep_rows, preferred_element_type=jnp.float32
        )
        angle_now = angle_now - correction.reshape(bus_count, hour_count)
        price_now = price_now + penalty * mismatch
        dispatch = dispatch_next
    return (
        angle_now[None],
        dispatch.astype(jnp.bfloat16)[None],
        price_now[None],
        charge_state[None],
    )


def solution(mesh):
    in_specs = (
        P("area", None, "tm"),
        P("area", None, "tm"),
        P("area", None, "tm"),
        P("area", None, None, "tm"),
        P("area", None, None),
        P("area", None, None, None),
        P("area", None),
        P("area", None),
        P(),
        P("area", None, None),
        P("area", None, None),
        P("area", None, None),
        P("area", None),
        P("area", None),
        P("area", None),
        P("area", None, "tm"),
    )
    out_specs = (
        P("area", None, "tm"),
        P("area", None, "tm"),
        P("area", None, None, "tm"),
        P("area", None, "tm"),
    )
    return jax.shard_map(local, mesh=mesh, in_specs=in_specs, out_specs=out_specs, check_vma=False)
```

```python
import math

import jax
import jax.numpy as jnp
from jax import lax
from jax.experimental import pallas as pl
from jax.experimental.pallas import tpu as pltpu
from jax.sharding import PartitionSpec as P

ITERS = 2


dispatch_step = 0.5


def padded_2(x, sides, width):
    for axis, dim in sides:
        size, length = (lax.axis_size(axis), x.shape[dim])
        up = [(i, (i + 1) % size) for i in range(size - 1)]
        down = [(j, i) for i, j in up]
        last = lax.slice_in_dim(x, length - width, length, axis=dim)
        leading = lax.slice_in_dim(x, 0, width, axis=dim)
        before = lax.ppermute(last, axis, up)
        after = lax.ppermute(leading, axis, down)
        x = jnp.concatenate([before, x, after], axis=dim)
    return x


def shifted_in(x, lane, step, fill):
    count = x.shape[1]
    ahead = pltpu.roll(x, step, 1)
    behind = pltpu.roll(x, count - step, 1)
    source = pltpu.roll(lane, step, 1)
    moved = jnp.where(source == lane - step, ahead, behind)
    return jnp.where(lane >= step, moved, fill)


def scan_kernel(kept_ref, charge_ref, total_ref, state_ref):
    kept = kept_ref[...]
    state = charge_ref[...]
    lane = lax.broadcasted_iota(jnp.int32, kept.shape, 1)
    step = 1
    while step < kept.shape[1]:
        state = kept * shifted_in(state, lane, step, 0.0) + state
        kept = kept * shifted_in(kept, lane, step, 1.0)
        step *= 2
    total_ref[...] = kept
    state_ref[...] = state


def window_scan(kept, charge):
    shape = jax.ShapeDtypeStruct(kept.shape, jnp.float32)
    return pl.pallas_call(scan_kernel, out_shape=(shape, shape))(kept, charge)


def carried_state(kept_last, state_last, position):
    state_in = jnp.zeros_like(state_last[0])
    for window in range(state_last.shape[0]):
        folded = kept_last[window] * state_in + state_last[window]
        state_in = jnp.where(window < position, folded, state_in)
    return state_in


def local(
    angle_start,
    dispatch_start,
    demand,
    price_start,
    susceptance,
    tile_inverse,
    cost_slope,
    ramp_weight,
    partner,
    boundary,
    tie_susceptance,
    tie_penalty,
    store_bus,
    store_gain,
    store_output,
    retention,
):
    area_count = lax.axis_size("area")
    area_here = lax.axis_index("area")
    position = lax.axis_index("tm")
    partners = jnp.take(partner, area_here, axis=1)
    edge_rows = boundary[0]
    store_rows = store_bus[0]
    matrix = susceptance[0]
    inverses = tile_inverse[0]
    tile_count = inverses.shape[0]
    tile_width = inverses.shape[1]
    bus_count = matrix.shape[0]
    hour_count = retention.shape[2]
    year_hours = hour_count * lax.axis_size("tm")
    kept_local = retention[0]
    angle_now = angle_start[0].astype(jnp.float32)
    dispatch = dispatch_start[0].astype(jnp.float32)
    price_now = price_start[0].astype(jnp.float32)
    demand_local = demand[0].astype(jnp.float32)
    tie_gain = tie_susceptance[0][:, :, None]
    penalty = tie_penalty[0][:, :, None]
    slope = cost_slope[0][:, None]
    ramp_local = ramp_weight[0][:, None]
    gain_local = store_gain[0][:, None]
    output_local = store_output[0][:, None]
    injection = jnp.zeros((bus_count, hour_count), jnp.float32)
    charge_state = jnp.zeros_like(kept_local)
    rounds, lines = edge_rows.shape

    slot_ids = jnp.arange(area_count, dtype=jnp.int32)
    round_ids = jnp.arange(rounds, dtype=jnp.int32)
    round_of = jnp.sum(jnp.where(partners[:, None] == slot_ids[None, :], round_ids[:, None], 0), axis=0)
    slot_rows = jnp.take(edge_rows, round_of, axis=0)

    def exchanged(parts, shapes):
        lanes = 128
        sent = jnp.concatenate([part.reshape(area_count, -1, lanes) for part in parts], axis=1)
        sent = jnp.pad(sent, ((0, 0), (0, -sent.shape[1] % 8), (0, 0)))
        got = lax.all_to_all(sent, "area", split_axis=0, concat_axis=0, tiled=True)
        got = jnp.take(got, partners, axis=0).reshape(rounds, -1)
        found, at = [], 0
        for shape in shapes:
            width = math.prod(shape[1:])
            found.append(got[:, at : at + width].reshape(shape))
            at += width
        return found

    kept_total = None
    price_far = None
    penalty_far = None
    mismatch = None
    for iteration in range(ITERS):
        rounded = angle_now.astype(jnp.bfloat16)
        own_edge = rounded[edge_rows].astype(jnp.float32)
        edge_out = rounded[slot_rows].astype(jnp.float32)
        if iteration == 0:
            far_edge, price_far, penalty_far = exchanged(
                (edge_out, jnp.take(price_now, round_of, axis=0),
                 jnp.take(tie_penalty[0], round_of, axis=0)),
                (own_edge.shape, price_now.shape, tie_penalty[0].shape),
            )
            penalty_far = penalty_far[:, :, None]
        else:
            (far_edge,) = exchanged((edge_out,), (own_edge.shape,))
            price_far = price_far - penalty_far * mismatch
        mismatch = own_edge - far_edge
        tie_flow = tie_gain * mismatch + 0.5 * (price_now - price_far)
        spread = jnp.zeros((bus_count, hour_count), jnp.float32).at[edge_rows].add(tie_flow)
        fixed_part = demand_local - dispatch - injection + spread
        balance = jnp.dot(matrix, rounded, preferred_element_type=jnp.float32) + fixed_part
        padded = padded_2(dispatch, (("tm", 1),), 1)
        bend = padded[:, :-2] - 2.0 * dispatch + padded[:, 2:]
        dispatch_next = dispatch + dispatch_step * (balance - slope * dispatch) + ramp_local * bend
        charge = -gain_local * balance[store_rows] / math.sqrt(year_hours)
        kept_total, local_state = window_scan(kept_local, charge)
        ends = jnp.stack([kept_total[:, -1], local_state[:, -1]])
        copies = jnp.broadcast_to(ends, (lax.axis_size("tm"),) + ends.shape)
        ends = lax.all_to_all(copies, "tm", split_axis=0, concat_axis=0, tiled=True)
        state_in = carried_state(ends[:, 0], ends[:, 1], position)
        charge_state = local_state + kept_total * state_in[:, None]
        injection = (
            jnp.zeros((bus_count, hour_count), jnp.float32)
            .at[store_rows]
            .add(output_local * charge_state)
        )
        sweep_rows = balance.astype(jnp.bfloat16).reshape(tile_count, tile_width, hour_count)
        correction = jnp.einsum(
            "tij,tjh->tih", inverses, sweep_rows, preferred_element_type=jnp.float32
        )
        angle_now = angle_now - correction.reshape(bus_count, hour_count)
        price_now = price_now + penalty * mismatch
        dispatch = dispatch_next
    return (
        angle_now[None],
        dispatch.astype(jnp.bfloat16)[None],
        price_now[None],
        charge_state[None],
    )


def solution(mesh):
    in_specs = (
        P("area", None, "tm"),
        P("area", None, "tm"),
        P("area", None, "tm"),
        P("area", None, None, "tm"),
        P("area", None, None),
        P("area", None, None, None),
        P("area", None),
        P("area", None),
        P(),
        P("area", None, None),
        P("area", None, None),
        P("area", None, None),
        P("area", None),
        P("area", None),
        P("area", None),
        P("area", None, "tm"),
    )
    out_specs = (
        P("area", None, "tm"),
        P("area", None, "tm"),
        P("area", None, None, "tm"),
        P("area", None, "tm"),
    )
    return jax.shard_map(local, mesh=mesh, in_specs=in_specs, out_specs=out_specs, check_vma=False)
```

```python
import math

import jax
import jax.numpy as jnp
from jax import lax
from jax.experimental import pallas as pl
from jax.experimental.pallas import tpu as pltpu
from jax.sharding import PartitionSpec as P

ITERS = 2


dispatch_step = 0.5


def padded_2(x, sides, width):
    for axis, dim in sides:
        size, length = (lax.axis_size(axis), x.shape[dim])
        up = [(i, (i + 1) % size) for i in range(size - 1)]
        down = [(j, i) for i, j in up]
        last = lax.slice_in_dim(x, length - width, length, axis=dim)
        leading = lax.slice_in_dim(x, 0, width, axis=dim)
        before = lax.ppermute(last, axis, up)
        after = lax.ppermute(leading, axis, down)
        x = jnp.concatenate([before, x, after], axis=dim)
    return x


def shifted_in(x, lane, step, fill):
    count = x.shape[1]
    ahead = pltpu.roll(x, step, 1)
    behind = pltpu.roll(x, count - step, 1)
    source = pltpu.roll(lane, step, 1)
    moved = jnp.where(source == lane - step, ahead, behind)
    return jnp.where(lane >= step, moved, fill)


def scan_kernel(kept_ref, charge_ref, total_ref, state_ref):
    kept = kept_ref[...]
    state = charge_ref[...]
    lane = lax.broadcasted_iota(jnp.int32, kept.shape, 1)
    step = 1
    while step < kept.shape[1]:
        state = kept * shifted_in(state, lane, step, 0.0) + state
        kept = kept * shifted_in(kept, lane, step, 1.0)
        step *= 2
    total_ref[...] = kept
    state_ref[...] = state


def window_scan(kept, charge):
    shape = jax.ShapeDtypeStruct(kept.shape, jnp.float32)
    return pl.pallas_call(scan_kernel, out_shape=(shape, shape))(kept, charge)


def carried_state(kept_last, state_last, position):
    state_in = jnp.zeros_like(state_last[0])
    for window in range(state_last.shape[0]):
        folded = kept_last[window] * state_in + state_last[window]
        state_in = jnp.where(window < position, folded, state_in)
    return state_in


def local(
    angle_start,
    dispatch_start,
    demand,
    price_start,
    susceptance,
    tile_inverse,
    cost_slope,
    ramp_weight,
    partner,
    boundary,
    tie_susceptance,
    tie_penalty,
    store_bus,
    store_gain,
    store_output,
    retention,
):
    area_count = lax.axis_size("area")
    area_here = lax.axis_index("area")
    position = lax.axis_index("tm")
    partners = jnp.take(partner, area_here, axis=1)
    edge_rows = boundary[0]
    store_rows = store_bus[0]
    matrix = susceptance[0]
    inverses = tile_inverse[0]
    tile_count = inverses.shape[0]
    tile_width = inverses.shape[1]
    bus_count = matrix.shape[0]
    hour_count = retention.shape[2]
    year_hours = hour_count * lax.axis_size("tm")
    kept_local = retention[0]
    angle_now = angle_start[0].astype(jnp.float32)
    dispatch = dispatch_start[0].astype(jnp.float32)
    price_now = price_start[0].astype(jnp.float32)
    demand_local = demand[0].astype(jnp.float32)
    tie_gain = tie_susceptance[0][:, :, None]
    penalty = tie_penalty[0][:, :, None]
    slope = cost_slope[0][:, None]
    ramp_local = ramp_weight[0][:, None]
    gain_local = store_gain[0][:, None]
    output_local = store_output[0][:, None]
    injection = jnp.zeros((bus_count, hour_count), jnp.float32)
    charge_state = jnp.zeros_like(kept_local)
    rounds, lines = edge_rows.shape

    slot_ids = jnp.arange(area_count, dtype=jnp.int32)
    round_ids = jnp.arange(rounds, dtype=jnp.int32)
    round_of = jnp.sum(jnp.where(partners[:, None] == slot_ids[None, :], round_ids[:, None], 0), axis=0)

    def exchanged(parts, shapes):
        lanes = 128
        sent = jnp.concatenate([part.reshape(area_count, -1, lanes) for part in parts], axis=1)
        sent = jnp.pad(sent, ((0, 0), (0, -sent.shape[1] % 8), (0, 0)))
        got = lax.all_to_all(sent, "area", split_axis=0, concat_axis=0, tiled=True)
        got = jnp.take(got, partners, axis=0).reshape(rounds, -1)
        found, at = [], 0
        for shape in shapes:
            width = math.prod(shape[1:])
            found.append(got[:, at : at + width].reshape(shape))
            at += width
        return found

    kept_total = None
    price_far = None
    penalty_far = None
    mismatch = None
    for iteration in range(ITERS):
        rounded = angle_now.astype(jnp.bfloat16)
        own_edge = lax.optimization_barrier(rounded[edge_rows].astype(jnp.float32))
        edge_out = jnp.take(own_edge, round_of, axis=0)
        if iteration == 0:
            far_edge, price_far, penalty_far = exchanged(
                (edge_out, jnp.take(price_now, round_of, axis=0),
                 jnp.take(tie_penalty[0], round_of, axis=0)),
                (own_edge.shape, price_now.shape, tie_penalty[0].shape),
            )
            penalty_far = penalty_far[:, :, None]
        else:
            (far_edge,) = exchanged((edge_out,), (own_edge.shape,))
            price_far = price_far - penalty_far * mismatch
        mismatch = own_edge - far_edge
        tie_flow = tie_gain * mismatch + 0.5 * (price_now - price_far)
        spread = jnp.zeros((bus_count, hour_count), jnp.float32).at[edge_rows].add(tie_flow)
        fixed_part = demand_local - dispatch - injection + spread
        balance = jnp.dot(matrix, rounded, preferred_element_type=jnp.float32) + fixed_part
        padded = padded_2(dispatch, (("tm", 1),), 1)
        bend = padded[:, :-2] - 2.0 * dispatch + padded[:, 2:]
        dispatch_next = dispatch + dispatch_step * (balance - slope * dispatch) + ramp_local * bend
        charge = -gain_local * balance[store_rows] / math.sqrt(year_hours)
        kept_total, local_state = window_scan(kept_local, charge)
        ends = jnp.stack([kept_total[:, -1], local_state[:, -1]])
        copies = jnp.broadcast_to(ends, (lax.axis_size("tm"),) + ends.shape)
        ends = lax.all_to_all(copies, "tm", split_axis=0, concat_axis=0, tiled=True)
        state_in = carried_state(ends[:, 0], ends[:, 1], position)
        charge_state = local_state + kept_total * state_in[:, None]
        injection = (
            jnp.zeros((bus_count, hour_count), jnp.float32)
            .at[store_rows]
            .add(output_local * charge_state)
        )
        sweep_rows = balance.astype(jnp.bfloat16).reshape(tile_count, tile_width, hour_count)
        correction = jnp.einsum(
            "tij,tjh->tih", inverses, sweep_rows, preferred_element_type=jnp.float32
        )
        angle_now = angle_now - correction.reshape(bus_count, hour_count)
        price_now = price_now + penalty * mismatch
        dispatch = dispatch_next
    return (
        angle_now[None],
        dispatch.astype(jnp.bfloat16)[None],
        price_now[None],
        charge_state[None],
    )


def solution(mesh):
    in_specs = (
        P("area", None, "tm"),
        P("area", None, "tm"),
        P("area", None, "tm"),
        P("area", None, None, "tm"),
        P("area", None, None),
        P("area", None, None, None),
        P("area", None),
        P("area", None),
        P(),
        P("area", None, None),
        P("area", None, None),
        P("area", None, None),
        P("area", None),
        P("area", None),
        P("area", None),
        P("area", None, "tm"),
    )
    out_specs = (
        P("area", None, "tm"),
        P("area", None, "tm"),
        P("area", None, None, "tm"),
        P("area", None, "tm"),
    )
    return jax.shard_map(local, mesh=mesh, in_specs=in_specs, out_specs=out_specs, check_vma=False)
```

```python
import math

import jax
import jax.numpy as jnp
from jax import lax
from jax.experimental import pallas as pl
from jax.experimental.pallas import tpu as pltpu
from jax.sharding import PartitionSpec as P

ITERS = 2


dispatch_step = 0.5


def padded_2(x, sides, width):
    for axis, dim in sides:
        size, length = (lax.axis_size(axis), x.shape[dim])
        up = [(i, (i + 1) % size) for i in range(size - 1)]
        down = [(j, i) for i, j in up]
        last = lax.slice_in_dim(x, length - width, length, axis=dim)
        leading = lax.slice_in_dim(x, 0, width, axis=dim)
        before = lax.ppermute(last, axis, up)
        after = lax.ppermute(leading, axis, down)
        x = jnp.concatenate([before, x, after], axis=dim)
    return x


def shifted_in(x, lane, step, fill):
    count = x.shape[1]
    ahead = pltpu.roll(x, step, 1)
    behind = pltpu.roll(x, count - step, 1)
    source = pltpu.roll(lane, step, 1)
    moved = jnp.where(source == lane - step, ahead, behind)
    return jnp.where(lane >= step, moved, fill)


def scan_kernel(kept_ref, charge_ref, total_ref, state_ref):
    kept = kept_ref[...]
    state = charge_ref[...]
    lane = lax.broadcasted_iota(jnp.int32, kept.shape, 1)
    step = 1
    while step < kept.shape[1]:
        state = kept * shifted_in(state, lane, step, 0.0) + state
        kept = kept * shifted_in(kept, lane, step, 1.0)
        step *= 2
    total_ref[...] = kept
    state_ref[...] = state


def window_scan(kept, charge):
    shape = jax.ShapeDtypeStruct(kept.shape, jnp.float32)
    return pl.pallas_call(scan_kernel, out_shape=(shape, shape))(kept, charge)


def spread_kernel(rows_ref, flow_ref, out_ref):
    block = out_ref.shape[0]
    first = pl.program_id(0) * block
    bus = first + lax.broadcasted_iota(jnp.int32, (block, rows_ref.shape[1]), 0)
    pick = (bus == rows_ref[...]).astype(jnp.float32)
    out_ref[...] = jnp.dot(
        pick, flow_ref[...], precision=lax.Precision.HIGHEST, preferred_element_type=jnp.float32
    )


def spread_rows(rows, flow, bus_count):
    block = bus_count // 8
    lines, hours = flow.shape
    return pl.pallas_call(
        spread_kernel,
        grid=(bus_count // block,),
        in_specs=[
            pl.BlockSpec((1, lines), lambda i: (0, 0)),
            pl.BlockSpec((lines, hours), lambda i: (0, 0)),
        ],
        out_specs=pl.BlockSpec((block, hours), lambda i: (i, 0)),
        out_shape=jax.ShapeDtypeStruct((bus_count, hours), jnp.float32),
    )(rows.reshape(1, lines), flow)


def carried_state(kept_last, state_last, position):
    state_in = jnp.zeros_like(state_last[0])
    for window in range(state_last.shape[0]):
        folded = kept_last[window] * state_in + state_last[window]
        state_in = jnp.where(window < position, folded, state_in)
    return state_in


def local(
    angle_start,
    dispatch_start,
    demand,
    price_start,
    susceptance,
    tile_inverse,
    cost_slope,
    ramp_weight,
    partner,
    boundary,
    tie_susceptance,
    tie_penalty,
    store_bus,
    store_gain,
    store_output,
    retention,
):
    area_count = lax.axis_size("area")
    area_here = lax.axis_index("area")
    position = lax.axis_index("tm")
    partners = jnp.take(partner, area_here, axis=1)
    edge_rows = boundary[0]
    store_rows = store_bus[0]
    matrix = susceptance[0]
    inverses = tile_inverse[0]
    tile_count = inverses.shape[0]
    tile_width = inverses.shape[1]
    bus_count = matrix.shape[0]
    hour_count = retention.shape[2]
    year_hours = hour_count * lax.axis_size("tm")
    kept_local = retention[0]
    angle_now = angle_start[0].astype(jnp.float32)
    dispatch = dispatch_start[0].astype(jnp.float32)
    price_now = price_start[0].astype(jnp.float32)
    demand_local = demand[0].astype(jnp.float32)
    tie_gain = tie_susceptance[0][:, :, None]
    penalty = tie_penalty[0][:, :, None]
    slope = cost_slope[0][:, None]
    ramp_local = ramp_weight[0][:, None]
    gain_local = store_gain[0][:, None]
    output_local = store_output[0][:, None]
    injection = jnp.zeros((bus_count, hour_count), jnp.float32)
    charge_state = jnp.zeros_like(kept_local)
    rounds, lines = edge_rows.shape

    slot_ids = jnp.arange(area_count, dtype=jnp.int32)
    round_ids = jnp.arange(rounds, dtype=jnp.int32)
    round_of = jnp.sum(jnp.where(partners[:, None] == slot_ids[None, :], round_ids[:, None], 0), axis=0)

    def exchanged(parts, shapes):
        lanes = 128
        sent = jnp.concatenate([part.reshape(area_count, -1, lanes) for part in parts], axis=1)
        sent = jnp.pad(sent, ((0, 0), (0, -sent.shape[1] % 8), (0, 0)))
        got = lax.all_to_all(sent, "area", split_axis=0, concat_axis=0, tiled=True)
        got = jnp.take(got, partners, axis=0).reshape(rounds, -1)
        found, at = [], 0
        for shape in shapes:
            width = math.prod(shape[1:])
            found.append(got[:, at : at + width].reshape(shape))
            at += width
        return found

    kept_total = None
    price_far = None
    penalty_far = None
    mismatch = None
    for iteration in range(ITERS):
        rounded = angle_now.astype(jnp.bfloat16)
        own_edge = lax.optimization_barrier(rounded[edge_rows].astype(jnp.float32))
        edge_out = jnp.take(own_edge, round_of, axis=0)
        if iteration == 0:
            far_edge, price_far, penalty_far = exchanged(
                (edge_out, jnp.take(price_now, round_of, axis=0),
                 jnp.take(tie_penalty[0], round_of, axis=0)),
                (own_edge.shape, price_now.shape, tie_penalty[0].shape),
            )
            penalty_far = penalty_far[:, :, None]
        else:
            (far_edge,) = exchanged((edge_out,), (own_edge.shape,))
            price_far = price_far - penalty_far * mismatch
        mismatch = own_edge - far_edge
        tie_flow = tie_gain * mismatch + 0.5 * (price_now - price_far)
        spread = spread_rows(edge_rows, tie_flow.reshape(rounds * lines, hour_count), bus_count)
        fixed_part = demand_local - dispatch - injection + spread
        balance = jnp.dot(matrix, rounded, preferred_element_type=jnp.float32) + fixed_part
        padded = padded_2(dispatch, (("tm", 1),), 1)
        bend = padded[:, :-2] - 2.0 * dispatch + padded[:, 2:]
        dispatch_next = dispatch + dispatch_step * (balance - slope * dispatch) + ramp_local * bend
        charge = -gain_local * balance[store_rows] / math.sqrt(year_hours)
        kept_total, local_state = window_scan(kept_local, charge)
        ends = jnp.stack([kept_total[:, -1], local_state[:, -1]])
        copies = jnp.broadcast_to(ends, (lax.axis_size("tm"),) + ends.shape)
        ends = lax.all_to_all(copies, "tm", split_axis=0, concat_axis=0, tiled=True)
        state_in = carried_state(ends[:, 0], ends[:, 1], position)
        charge_state = local_state + kept_total * state_in[:, None]
        injection = (
            jnp.zeros((bus_count, hour_count), jnp.float32)
            .at[store_rows]
            .add(output_local * charge_state)
        )
        sweep_rows = balance.astype(jnp.bfloat16).reshape(tile_count, tile_width, hour_count)
        correction = jnp.einsum(
            "tij,tjh->tih", inverses, sweep_rows, preferred_element_type=jnp.float32
        )
        angle_now = angle_now - correction.reshape(bus_count, hour_count)
        price_now = price_now + penalty * mismatch
        dispatch = dispatch_next
    return (
        angle_now[None],
        dispatch.astype(jnp.bfloat16)[None],
        price_now[None],
        charge_state[None],
    )


def solution(mesh):
    in_specs = (
        P("area", None, "tm"),
        P("area", None, "tm"),
        P("area", None, "tm"),
        P("area", None, None, "tm"),
        P("area", None, None),
        P("area", None, None, None),
        P("area", None),
        P("area", None),
        P(),
        P("area", None, None),
        P("area", None, None),
        P("area", None, None),
        P("area", None),
        P("area", None),
        P("area", None),
        P("area", None, "tm"),
    )
    out_specs = (
        P("area", None, "tm"),
        P("area", None, "tm"),
        P("area", None, None, "tm"),
        P("area", None, "tm"),
    )
    return jax.shard_map(local, mesh=mesh, in_specs=in_specs, out_specs=out_specs, check_vma=False)
```

```python
import math

import jax
import jax.numpy as jnp
from jax import lax
from jax.experimental import pallas as pl
from jax.experimental.pallas import tpu as pltpu
from jax.sharding import PartitionSpec as P

ITERS = 2


dispatch_step = 0.5


def padded_2(x, sides, width):
    for axis, dim in sides:
        size, length = (lax.axis_size(axis), x.shape[dim])
        up = [(i, (i + 1) % size) for i in range(size - 1)]
        down = [(j, i) for i, j in up]
        last = lax.slice_in_dim(x, length - width, length, axis=dim)
        leading = lax.slice_in_dim(x, 0, width, axis=dim)
        before = lax.ppermute(last, axis, up)
        after = lax.ppermute(leading, axis, down)
        x = jnp.concatenate([before, x, after], axis=dim)
    return x


def shifted_in(x, lane, step, fill):
    count = x.shape[1]
    ahead = pltpu.roll(x, step, 1)
    behind = pltpu.roll(x, count - step, 1)
    source = pltpu.roll(lane, step, 1)
    moved = jnp.where(source == lane - step, ahead, behind)
    return jnp.where(lane >= step, moved, fill)


def scan_kernel(kept_ref, charge_ref, total_ref, state_ref):
    kept = kept_ref[...]
    state = charge_ref[...]
    lane = lax.broadcasted_iota(jnp.int32, kept.shape, 1)
    step = 1
    while step < kept.shape[1]:
        state = kept * shifted_in(state, lane, step, 0.0) + state
        kept = kept * shifted_in(kept, lane, step, 1.0)
        step *= 2
    total_ref[...] = kept
    state_ref[...] = state


def window_scan(kept, charge):
    shape = jax.ShapeDtypeStruct(kept.shape, jnp.float32)
    return pl.pallas_call(scan_kernel, out_shape=(shape, shape))(kept, charge)


def carried_state(kept_last, state_last, position):
    state_in = jnp.zeros_like(state_last[0])
    for window in range(state_last.shape[0]):
        folded = kept_last[window] * state_in + state_last[window]
        state_in = jnp.where(window < position, folded, state_in)
    return state_in


def local(
    angle_start,
    dispatch_start,
    demand,
    price_start,
    susceptance,
    tile_inverse,
    cost_slope,
    ramp_weight,
    partner,
    boundary,
    tie_susceptance,
    tie_penalty,
    store_bus,
    store_gain,
    store_output,
    retention,
):
    area_count = lax.axis_size("area")
    area_here = lax.axis_index("area")
    position = lax.axis_index("tm")
    partners = jnp.take(partner, area_here, axis=1)
    edge_rows = boundary[0]
    store_rows = store_bus[0]
    matrix = susceptance[0]
    inverses = tile_inverse[0]
    tile_count = inverses.shape[0]
    tile_width = inverses.shape[1]
    bus_count = matrix.shape[0]
    hour_count = retention.shape[2]
    year_hours = hour_count * lax.axis_size("tm")
    kept_local = retention[0]
    angle_now = angle_start[0].astype(jnp.float32)
    dispatch = dispatch_start[0].astype(jnp.float32)
    price_now = price_start[0].astype(jnp.float32)
    demand_local = demand[0].astype(jnp.float32)
    tie_gain = tie_susceptance[0][:, :, None]
    penalty = tie_penalty[0][:, :, None]
    slope = cost_slope[0][:, None]
    ramp_local = ramp_weight[0][:, None]
    gain_local = store_gain[0][:, None]
    output_local = store_output[0][:, None]
    injection = jnp.zeros((bus_count, hour_count), jnp.float32)
    charge_state = jnp.zeros_like(kept_local)
    rounds, lines = edge_rows.shape

    slot_ids = jnp.arange(area_count, dtype=jnp.int32)
    round_ids = jnp.arange(rounds, dtype=jnp.int32)
    round_of = jnp.sum(jnp.where(partners[:, None] == slot_ids[None, :], round_ids[:, None], 0), axis=0)

    def exchanged(parts, shapes):
        lanes = 128
        sent = jnp.concatenate([part.reshape(area_count, -1, lanes) for part in parts], axis=1)
        sent = jnp.pad(sent, ((0, 0), (0, -sent.shape[1] % 8), (0, 0)))
        got = lax.all_to_all(sent, "area", split_axis=0, concat_axis=0, tiled=True)
        got = jnp.take(got, partners, axis=0).reshape(rounds, -1)
        found, at = [], 0
        for shape in shapes:
            width = math.prod(shape[1:])
            found.append(got[:, at : at + width].reshape(shape))
            at += width
        return found

    bus_ids = lax.broadcasted_iota(jnp.int32, (1, bus_count), 1)
    edge_pick = (edge_rows.reshape(-1, 1) == bus_ids).astype(jnp.bfloat16)

    def spread_rows(pick, flow):
        high = lax.reduce_precision(flow, exponent_bits=8, mantissa_bits=7)
        middle = lax.reduce_precision(flow - high, exponent_bits=8, mantissa_bits=7)
        low = flow - high - middle
        parts = jnp.concatenate([high, middle, low], axis=1).astype(jnp.bfloat16)
        summed = lax.dot_general(
            pick, parts, (((0,), (0,)), ((), ())), preferred_element_type=jnp.float32
        )
        width = flow.shape[1]
        return summed[:, :width] + summed[:, width : 2 * width] + summed[:, 2 * width :]

    kept_total = None
    price_far = None
    penalty_far = None
    mismatch = None
    for iteration in range(ITERS):
        rounded = angle_now.astype(jnp.bfloat16)
        own_edge = jnp.dot(edge_pick, rounded, preferred_element_type=jnp.float32)
        own_edge = lax.optimization_barrier(own_edge.reshape(rounds, lines, hour_count))
        edge_out = jnp.take(own_edge, round_of, axis=0)
        if iteration == 0:
            far_edge, price_far, penalty_far = exchanged(
                (edge_out, jnp.take(price_now, round_of, axis=0),
                 jnp.take(tie_penalty[0], round_of, axis=0)),
                (own_edge.shape, price_now.shape, tie_penalty[0].shape),
            )
            penalty_far = penalty_far[:, :, None]
        else:
            (far_edge,) = exchanged((edge_out,), (own_edge.shape,))
            price_far = price_far - penalty_far * mismatch
        mismatch = own_edge - far_edge
        tie_flow = tie_gain * mismatch + 0.5 * (price_now - price_far)
        spread = spread_rows(edge_pick, tie_flow.reshape(rounds * lines, hour_count))
        fixed_part = demand_local - dispatch - injection + spread
        balance = jnp.dot(matrix, rounded, preferred_element_type=jnp.float32) + fixed_part
        padded = padded_2(dispatch, (("tm", 1),), 1)
        bend = padded[:, :-2] - 2.0 * dispatch + padded[:, 2:]
        dispatch_next = dispatch + dispatch_step * (balance - slope * dispatch) + ramp_local * bend
        charge = -gain_local * balance[store_rows] / math.sqrt(year_hours)
        kept_total, local_state = window_scan(kept_local, charge)
        ends = jnp.stack([kept_total[:, -1], local_state[:, -1]])
        copies = jnp.broadcast_to(ends, (lax.axis_size("tm"),) + ends.shape)
        ends = lax.all_to_all(copies, "tm", split_axis=0, concat_axis=0, tiled=True)
        state_in = carried_state(ends[:, 0], ends[:, 1], position)
        charge_state = local_state + kept_total * state_in[:, None]
        injection = (
            jnp.zeros((bus_count, hour_count), jnp.float32)
            .at[store_rows]
            .add(output_local * charge_state)
        )
        sweep_rows = balance.astype(jnp.bfloat16).reshape(tile_count, tile_width, hour_count)
        correction = jnp.einsum(
            "tij,tjh->tih", inverses, sweep_rows, preferred_element_type=jnp.float32
        )
        angle_now = angle_now - correction.reshape(bus_count, hour_count)
        price_now = price_now + penalty * mismatch
        dispatch = dispatch_next
    return (
        angle_now[None],
        dispatch.astype(jnp.bfloat16)[None],
        price_now[None],
        charge_state[None],
    )


def solution(mesh):
    in_specs = (
        P("area", None, "tm"),
        P("area", None, "tm"),
        P("area", None, "tm"),
        P("area", None, None, "tm"),
        P("area", None, None),
        P("area", None, None, None),
        P("area", None),
        P("area", None),
        P(),
        P("area", None, None),
        P("area", None, None),
        P("area", None, None),
        P("area", None),
        P("area", None),
        P("area", None),
        P("area", None, "tm"),
    )
    out_specs = (
        P("area", None, "tm"),
        P("area", None, "tm"),
        P("area", None, None, "tm"),
        P("area", None, "tm"),
    )
    return jax.shard_map(local, mesh=mesh, in_specs=in_specs, out_specs=out_specs, check_vma=False)
```

```python
import math

import jax
import jax.numpy as jnp
from jax import lax
from jax.experimental import pallas as pl
from jax.experimental.pallas import tpu as pltpu
from jax.sharding import PartitionSpec as P

ITERS = 2


dispatch_step = 0.5


def padded_2(x, sides, width):
    for axis, dim in sides:
        size, length = (lax.axis_size(axis), x.shape[dim])
        up = [(i, (i + 1) % size) for i in range(size - 1)]
        down = [(j, i) for i, j in up]
        last = lax.slice_in_dim(x, length - width, length, axis=dim)
        leading = lax.slice_in_dim(x, 0, width, axis=dim)
        before = lax.ppermute(last, axis, up)
        after = lax.ppermute(leading, axis, down)
        x = jnp.concatenate([before, x, after], axis=dim)
    return x


def shifted_in(x, lane, step, fill):
    count = x.shape[1]
    ahead = pltpu.roll(x, step, 1)
    behind = pltpu.roll(x, count - step, 1)
    source = pltpu.roll(lane, step, 1)
    moved = jnp.where(source == lane - step, ahead, behind)
    return jnp.where(lane >= step, moved, fill)


def scan_kernel(kept_ref, charge_ref, total_ref, state_ref):
    kept = kept_ref[...]
    state = charge_ref[...]
    lane = lax.broadcasted_iota(jnp.int32, kept.shape, 1)
    step = 1
    while step < kept.shape[1]:
        state = kept * shifted_in(state, lane, step, 0.0) + state
        kept = kept * shifted_in(kept, lane, step, 1.0)
        step *= 2
    total_ref[...] = kept
    state_ref[...] = state


def window_scan(kept, charge):
    shape = jax.ShapeDtypeStruct(kept.shape, jnp.float32)
    return pl.pallas_call(scan_kernel, out_shape=(shape, shape))(kept, charge)


def carried_state(kept_last, state_last, position):
    state_in = jnp.zeros_like(state_last[0])
    for window in range(state_last.shape[0]):
        folded = kept_last[window] * state_in + state_last[window]
        state_in = jnp.where(window < position, folded, state_in)
    return state_in


def local(
    angle_start,
    dispatch_start,
    demand,
    price_start,
    susceptance,
    tile_inverse,
    cost_slope,
    ramp_weight,
    partner,
    boundary,
    tie_susceptance,
    tie_penalty,
    store_bus,
    store_gain,
    store_output,
    retention,
):
    area_count = lax.axis_size("area")
    area_here = lax.axis_index("area")
    position = lax.axis_index("tm")
    partners = jnp.take(partner, area_here, axis=1, mode="clip")
    edge_rows = boundary[0]
    store_rows = store_bus[0]
    matrix = susceptance[0]
    inverses = tile_inverse[0]
    tile_count = inverses.shape[0]
    tile_width = inverses.shape[1]
    bus_count = matrix.shape[0]
    hour_count = retention.shape[2]
    year_hours = hour_count * lax.axis_size("tm")
    kept_local = retention[0]
    angle_now = angle_start[0].astype(jnp.float32)
    dispatch = dispatch_start[0].astype(jnp.float32)
    price_now = price_start[0].astype(jnp.float32)
    demand_local = demand[0].astype(jnp.float32)
    tie_gain = tie_susceptance[0][:, :, None]
    penalty = tie_penalty[0][:, :, None]
    slope = cost_slope[0][:, None]
    ramp_local = ramp_weight[0][:, None]
    gain_local = store_gain[0][:, None]
    output_local = store_output[0][:, None]
    injection = jnp.zeros((bus_count, hour_count), jnp.float32)
    charge_state = jnp.zeros_like(kept_local)
    rounds, lines = edge_rows.shape

    slot_ids = jnp.arange(area_count, dtype=jnp.int32)
    round_ids = jnp.arange(rounds, dtype=jnp.int32)
    round_of = jnp.sum(jnp.where(partners[:, None] == slot_ids[None, :], round_ids[:, None], 0), axis=0)

    def exchanged(parts, shapes):
        lanes = 128
        blocks = [part.reshape(rounds, -1, lanes) for part in parts]
        blocks = [jnp.pad(b, ((0, 0), (0, -b.shape[1] % 8), (0, 0))) for b in blocks]
        sent = jnp.take(jnp.concatenate(blocks, axis=1), round_of, axis=0, mode="clip")
        got = lax.all_to_all(sent, "area", split_axis=0, concat_axis=0, tiled=True)
        got = jnp.take(got, partners, axis=0, mode="clip").reshape(rounds, -1)
        found, at = [], 0
        for shape in shapes:
            width = math.prod(shape[1:])
            found.append(got[:, at : at + width].reshape(shape))
            at += width
        return found

    kept_total = None
    price_far = None
    penalty_far = None
    mismatch = None
    for iteration in range(ITERS):
        rounded = angle_now.astype(jnp.bfloat16)
        own_edge = lax.optimization_barrier(rounded[edge_rows].astype(jnp.float32))
        if iteration == 0:
            far_edge, price_far, penalty_far = exchanged(
                (own_edge, price_now, tie_penalty[0]),
                (own_edge.shape, price_now.shape, tie_penalty[0].shape),
            )
            penalty_far = penalty_far[:, :, None]
        else:
            (far_edge,) = exchanged((own_edge,), (own_edge.shape,))
            price_far = price_far - penalty_far * mismatch
        mismatch = own_edge - far_edge
        tie_flow = tie_gain * mismatch + 0.5 * (price_now - price_far)
        spread = jnp.zeros((bus_count, hour_count), jnp.float32).at[edge_rows].add(tie_flow)
        fixed_part = demand_local - dispatch - injection + spread
        balance = jnp.dot(matrix, rounded, preferred_element_type=jnp.float32) + fixed_part
        padded = padded_2(dispatch, (("tm", 1),), 1)
        bend = padded[:, :-2] - 2.0 * dispatch + padded[:, 2:]
        dispatch_next = dispatch + dispatch_step * (balance - slope * dispatch) + ramp_local * bend
        charge = -gain_local * balance[store_rows] / math.sqrt(year_hours)
        kept_total, local_state = window_scan(kept_local, charge)
        ends = jnp.stack([kept_total[:, -1], local_state[:, -1]])
        copies = jnp.broadcast_to(ends, (lax.axis_size("tm"),) + ends.shape)
        ends = lax.all_to_all(copies, "tm", split_axis=0, concat_axis=0, tiled=True)
        state_in = carried_state(ends[:, 0], ends[:, 1], position)
        charge_state = local_state + kept_total * state_in[:, None]
        injection = (
            jnp.zeros((bus_count, hour_count), jnp.float32)
            .at[store_rows]
            .add(output_local * charge_state)
        )
        sweep_rows = balance.astype(jnp.bfloat16).reshape(tile_count, tile_width, hour_count)
        correction = jnp.einsum(
            "tij,tjh->tih", inverses, sweep_rows, preferred_element_type=jnp.float32
        )
        angle_now = angle_now - correction.reshape(bus_count, hour_count)
        price_now = price_now + penalty * mismatch
        dispatch = dispatch_next
    return (
        angle_now[None],
        dispatch.astype(jnp.bfloat16)[None],
        price_now[None],
        charge_state[None],
    )


def solution(mesh):
    in_specs = (
        P("area", None, "tm"),
        P("area", None, "tm"),
        P("area", None, "tm"),
        P("area", None, None, "tm"),
        P("area", None, None),
        P("area", None, None, None),
        P("area", None),
        P("area", None),
        P(),
        P("area", None, None),
        P("area", None, None),
        P("area", None, None),
        P("area", None),
        P("area", None),
        P("area", None),
        P("area", None, "tm"),
    )
    out_specs = (
        P("area", None, "tm"),
        P("area", None, "tm"),
        P("area", None, None, "tm"),
        P("area", None, "tm"),
    )
    return jax.shard_map(local, mesh=mesh, in_specs=in_specs, out_specs=out_specs, check_vma=False)
```

```python
import math

import jax
import jax.numpy as jnp
from jax import lax
from jax.experimental import pallas as pl
from jax.experimental.pallas import tpu as pltpu
from jax.sharding import PartitionSpec as P

ITERS = 2


dispatch_step = 0.5


def padded_2(x, sides, width):
    for axis, dim in sides:
        size, length = (lax.axis_size(axis), x.shape[dim])
        up = [(i, (i + 1) % size) for i in range(size - 1)]
        down = [(j, i) for i, j in up]
        last = lax.slice_in_dim(x, length - width, length, axis=dim)
        leading = lax.slice_in_dim(x, 0, width, axis=dim)
        before = lax.ppermute(last, axis, up)
        after = lax.ppermute(leading, axis, down)
        x = jnp.concatenate([before, x, after], axis=dim)
    return x


def shifted_in(x, lane, step, fill):
    count = x.shape[1]
    ahead = pltpu.roll(x, step, 1)
    behind = pltpu.roll(x, count - step, 1)
    source = pltpu.roll(lane, step, 1)
    moved = jnp.where(source == lane - step, ahead, behind)
    return jnp.where(lane >= step, moved, fill)


def scan_kernel(kept_ref, charge_ref, total_ref, state_ref, ends_ref):
    kept = kept_ref[...]
    state = charge_ref[...]
    lane = lax.broadcasted_iota(jnp.int32, kept.shape, 1)
    step = 1
    while step < kept.shape[1]:
        state = kept * shifted_in(state, lane, step, 0.0) + state
        kept = kept * shifted_in(kept, lane, step, 1.0)
        step *= 2
    total_ref[...] = kept
    state_ref[...] = state
    row = lax.broadcasted_iota(jnp.int32, ends_ref.shape, 1)
    kept_end = jnp.broadcast_to(jnp.transpose(kept)[-1:, :][None], ends_ref.shape)
    state_end = jnp.broadcast_to(jnp.transpose(state)[-1:, :][None], ends_ref.shape)
    ends_ref[...] = jnp.where(row == 0, kept_end, jnp.where(row == 1, state_end, 0.0))


def window_scan(kept, charge, copies):
    shape = jax.ShapeDtypeStruct(kept.shape, jnp.float32)
    ends = jax.ShapeDtypeStruct((copies, 8, kept.shape[0]), jnp.float32)
    return pl.pallas_call(scan_kernel, out_shape=(shape, shape, ends))(kept, charge)


def carried_state(kept_last, state_last, position):
    state_in = jnp.zeros_like(state_last[0])
    for window in range(state_last.shape[0]):
        folded = kept_last[window] * state_in + state_last[window]
        state_in = jnp.where(window < position, folded, state_in)
    return state_in


def local(
    angle_start,
    dispatch_start,
    demand,
    price_start,
    susceptance,
    tile_inverse,
    cost_slope,
    ramp_weight,
    partner,
    boundary,
    tie_susceptance,
    tie_penalty,
    store_bus,
    store_gain,
    store_output,
    retention,
):
    area_count = lax.axis_size("area")
    area_here = lax.axis_index("area")
    position = lax.axis_index("tm")
    partners = jnp.take(partner, area_here, axis=1, mode="clip")
    edge_rows = boundary[0]
    store_rows = store_bus[0]
    matrix = susceptance[0]
    inverses = tile_inverse[0]
    tile_count = inverses.shape[0]
    tile_width = inverses.shape[1]
    bus_count = matrix.shape[0]
    hour_count = retention.shape[2]
    year_hours = hour_count * lax.axis_size("tm")
    kept_local = retention[0]
    angle_now = angle_start[0].astype(jnp.float32)
    dispatch = dispatch_start[0].astype(jnp.float32)
    price_now = price_start[0].astype(jnp.float32)
    demand_local = demand[0].astype(jnp.float32)
    tie_gain = tie_susceptance[0][:, :, None]
    penalty = tie_penalty[0][:, :, None]
    slope = cost_slope[0][:, None]
    ramp_local = ramp_weight[0][:, None]
    gain_local = store_gain[0][:, None]
    output_local = store_output[0][:, None]
    injection = jnp.zeros((bus_count, hour_count), jnp.float32)
    charge_state = jnp.zeros_like(kept_local)
    rounds, lines = edge_rows.shape

    slot_ids = jnp.arange(area_count, dtype=jnp.int32)
    round_ids = jnp.arange(rounds, dtype=jnp.int32)
    round_of = jnp.sum(jnp.where(partners[:, None] == slot_ids[None, :], round_ids[:, None], 0), axis=0)

    def exchanged(parts, shapes):
        lanes = 128
        blocks = [part.reshape(rounds, -1, lanes) for part in parts]
        blocks = [jnp.pad(b, ((0, 0), (0, -b.shape[1] % 8), (0, 0))) for b in blocks]
        sent = jnp.take(jnp.concatenate(blocks, axis=1), round_of, axis=0, mode="clip")
        got = lax.all_to_all(sent, "area", split_axis=0, concat_axis=0, tiled=True)
        got = jnp.take(got, partners, axis=0, mode="clip").reshape(rounds, -1)
        found, at = [], 0
        for shape in shapes:
            width = math.prod(shape[1:])
            found.append(got[:, at : at + width].reshape(shape))
            at += width
        return found

    kept_total = None
    price_far = None
    penalty_far = None
    mismatch = None
    for iteration in range(ITERS):
        rounded = angle_now.astype(jnp.bfloat16)
        own_edge = lax.optimization_barrier(rounded[edge_rows].astype(jnp.float32))
        if iteration == 0:
            far_edge, price_far, penalty_far = exchanged(
                (own_edge, price_now, tie_penalty[0]),
                (own_edge.shape, price_now.shape, tie_penalty[0].shape),
            )
            penalty_far = penalty_far[:, :, None]
        else:
            (far_edge,) = exchanged((own_edge,), (own_edge.shape,))
            price_far = price_far - penalty_far * mismatch
        mismatch = own_edge - far_edge
        tie_flow = tie_gain * mismatch + 0.5 * (price_now - price_far)
        spread = jnp.zeros((bus_count, hour_count), jnp.float32).at[edge_rows].add(tie_flow)
        fixed_part = demand_local - dispatch - injection + spread
        balance = jnp.dot(matrix, rounded, preferred_element_type=jnp.float32) + fixed_part
        padded = padded_2(dispatch, (("tm", 1),), 1)
        bend = padded[:, :-2] - 2.0 * dispatch + padded[:, 2:]
        dispatch_next = dispatch + dispatch_step * (balance - slope * dispatch) + ramp_local * bend
        charge = -gain_local * balance[store_rows] / math.sqrt(year_hours)
        kept_total, local_state, copies = window_scan(kept_local, charge, lax.axis_size("tm"))
        ends = lax.all_to_all(copies, "tm", split_axis=0, concat_axis=0, tiled=True)
        state_in = carried_state(ends[:, 0], ends[:, 1], position)
        charge_state = local_state + kept_total * state_in[:, None]
        injection = (
            jnp.zeros((bus_count, hour_count), jnp.float32)
            .at[store_rows]
            .add(output_local * charge_state)
        )
        sweep_rows = balance.astype(jnp.bfloat16).reshape(tile_count, tile_width, hour_count)
        correction = jnp.einsum(
            "tij,tjh->tih", inverses, sweep_rows, preferred_element_type=jnp.float32
        )
        angle_now = angle_now - correction.reshape(bus_count, hour_count)
        price_now = price_now + penalty * mismatch
        dispatch = dispatch_next
    return (
        angle_now[None],
        dispatch.astype(jnp.bfloat16)[None],
        price_now[None],
        charge_state[None],
    )


def solution(mesh):
    in_specs = (
        P("area", None, "tm"),
        P("area", None, "tm"),
        P("area", None, "tm"),
        P("area", None, None, "tm"),
        P("area", None, None),
        P("area", None, None, None),
        P("area", None),
        P("area", None),
        P(),
        P("area", None, None),
        P("area", None, None),
        P("area", None, None),
        P("area", None),
        P("area", None),
        P("area", None),
        P("area", None, "tm"),
    )
    out_specs = (
        P("area", None, "tm"),
        P("area", None, "tm"),
        P("area", None, None, "tm"),
        P("area", None, "tm"),
    )
    return jax.shard_map(local, mesh=mesh, in_specs=in_specs, out_specs=out_specs, check_vma=False)
```

```python
import math

import jax
import jax.numpy as jnp
from jax import lax
from jax.experimental import pallas as pl
from jax.experimental.pallas import tpu as pltpu
from jax.sharding import PartitionSpec as P

ITERS = 2


dispatch_step = 0.5


def padded_2(x, sides, width):
    for axis, dim in sides:
        size, length = (lax.axis_size(axis), x.shape[dim])
        up = [(i, (i + 1) % size) for i in range(size - 1)]
        down = [(j, i) for i, j in up]
        last = lax.slice_in_dim(x, length - width, length, axis=dim)
        leading = lax.slice_in_dim(x, 0, width, axis=dim)
        before = lax.ppermute(last, axis, up)
        after = lax.ppermute(leading, axis, down)
        x = jnp.concatenate([before, x, after], axis=dim)
    return x


def shifted_in(x, lane, step, fill):
    count = x.shape[1]
    ahead = pltpu.roll(x, step, 1)
    behind = pltpu.roll(x, count - step, 1)
    source = pltpu.roll(lane, step, 1)
    moved = jnp.where(source == lane - step, ahead, behind)
    return jnp.where(lane >= step, moved, fill)


def scan_kernel(kept_ref, charge_ref, total_ref, state_ref, ends_ref):
    kept = kept_ref[...]
    state = charge_ref[...]
    lane = lax.broadcasted_iota(jnp.int32, kept.shape, 1)
    step = 1
    while step < kept.shape[1]:
        state = kept * shifted_in(state, lane, step, 0.0) + state
        kept = kept * shifted_in(kept, lane, step, 1.0)
        step *= 2
    total_ref[...] = kept
    state_ref[...] = state
    row = lax.broadcasted_iota(jnp.int32, ends_ref.shape, 1)
    kept_end = jnp.broadcast_to(jnp.transpose(kept)[-1:, :][None], ends_ref.shape)
    state_end = jnp.broadcast_to(jnp.transpose(state)[-1:, :][None], ends_ref.shape)
    ends_ref[...] = jnp.where(row == 0, kept_end, jnp.where(row == 1, state_end, 0.0))


def window_scan(kept, charge, copies):
    shape = jax.ShapeDtypeStruct(kept.shape, jnp.float32)
    ends = jax.ShapeDtypeStruct((copies, 8, kept.shape[0]), jnp.float32)
    return pl.pallas_call(scan_kernel, out_shape=(shape, shape, ends))(kept, charge)


def carried_state(kept_last, state_last, position):
    state_in = jnp.zeros_like(state_last[0])
    for window in range(state_last.shape[0]):
        folded = kept_last[window] * state_in + state_last[window]
        state_in = jnp.where(window < position, folded, state_in)
    return state_in


def local(
    angle_start,
    dispatch_start,
    demand,
    price_start,
    susceptance,
    tile_inverse,
    cost_slope,
    ramp_weight,
    partner,
    boundary,
    tie_susceptance,
    tie_penalty,
    store_bus,
    store_gain,
    store_output,
    retention,
):
    area_count = lax.axis_size("area")
    area_here = lax.axis_index("area")
    position = lax.axis_index("tm")
    partners = jnp.take(partner, area_here, axis=1, mode="clip")
    edge_rows = boundary[0]
    store_rows = store_bus[0]
    matrix = susceptance[0]
    inverses = tile_inverse[0]
    tile_count = inverses.shape[0]
    tile_width = inverses.shape[1]
    bus_count = matrix.shape[0]
    hour_count = retention.shape[2]
    year_hours = hour_count * lax.axis_size("tm")
    kept_local = retention[0]
    angle_now = angle_start[0].astype(jnp.float32)
    dispatch = dispatch_start[0].astype(jnp.float32)
    price_now = price_start[0].astype(jnp.float32)
    demand_local = demand[0].astype(jnp.float32)
    tie_gain = tie_susceptance[0][:, :, None]
    penalty = tie_penalty[0][:, :, None]
    slope = cost_slope[0][:, None]
    ramp_local = ramp_weight[0][:, None]
    gain_local = store_gain[0][:, None]
    output_local = store_output[0][:, None]
    injection = jnp.zeros((bus_count, hour_count), jnp.float32)
    charge_state = jnp.zeros_like(kept_local)
    rounds, lines = edge_rows.shape

    slot_ids = jnp.arange(area_count, dtype=jnp.int32)
    round_ids = jnp.arange(rounds, dtype=jnp.int32)
    round_of = jnp.sum(jnp.where(partners[:, None] == slot_ids[None, :], round_ids[:, None], 0), axis=0)

    def exchanged(parts, shapes):
        lanes = 128
        blocks = [part.reshape(rounds, -1, lanes) for part in parts]
        blocks = [jnp.pad(b, ((0, 0), (0, -b.shape[1] % 8), (0, 0))) for b in blocks]
        sent = jnp.take(jnp.concatenate(blocks, axis=1), round_of, axis=0, mode="clip")
        got = lax.all_to_all(sent, "area", split_axis=0, concat_axis=0, tiled=True)
        got = jnp.take(got, partners, axis=0, mode="clip").reshape(rounds, -1)
        found, at = [], 0
        for shape in shapes:
            width = math.prod(shape[1:])
            found.append(got[:, at : at + width].reshape(shape))
            at += width
        return found

    kept_total = None
    price_far = None
    penalty_far = None
    mismatch = None
    for iteration in range(ITERS):
        rounded = angle_now.astype(jnp.bfloat16)
        own_edge = lax.optimization_barrier(rounded.astype(jnp.float32)[edge_rows])
        if iteration == 0:
            far_edge, price_far, penalty_far = exchanged(
                (own_edge, price_now, tie_penalty[0]),
                (own_edge.shape, price_now.shape, tie_penalty[0].shape),
            )
            penalty_far = penalty_far[:, :, None]
        else:
            (far_edge,) = exchanged((own_edge,), (own_edge.shape,))
            price_far = price_far - penalty_far * mismatch
        mismatch = own_edge - far_edge
        tie_flow = tie_gain * mismatch + 0.5 * (price_now - price_far)
        spread = jnp.zeros((bus_count, hour_count), jnp.float32).at[edge_rows].add(tie_flow)
        fixed_part = demand_local - dispatch - injection + spread
        balance = jnp.dot(matrix, rounded, preferred_element_type=jnp.float32) + fixed_part
        padded = padded_2(dispatch, (("tm", 1),), 1)
        bend = padded[:, :-2] - 2.0 * dispatch + padded[:, 2:]
        dispatch_next = dispatch + dispatch_step * (balance - slope * dispatch) + ramp_local * bend
        charge = -gain_local * balance[store_rows] / math.sqrt(year_hours)
        kept_total, local_state, copies = window_scan(kept_local, charge, lax.axis_size("tm"))
        ends = lax.all_to_all(copies, "tm", split_axis=0, concat_axis=0, tiled=True)
        state_in = carried_state(ends[:, 0], ends[:, 1], position)
        charge_state = local_state + kept_total * state_in[:, None]
        injection = (
            jnp.zeros((bus_count, hour_count), jnp.float32)
            .at[store_rows]
            .add(output_local * charge_state)
        )
        sweep_rows = balance.astype(jnp.bfloat16).reshape(tile_count, tile_width, hour_count)
        correction = jnp.einsum(
            "tij,tjh->tih", inverses, sweep_rows, preferred_element_type=jnp.float32
        )
        angle_now = angle_now - correction.reshape(bus_count, hour_count)
        price_now = price_now + penalty * mismatch
        dispatch = dispatch_next
    return (
        angle_now[None],
        dispatch.astype(jnp.bfloat16)[None],
        price_now[None],
        charge_state[None],
    )


def solution(mesh):
    in_specs = (
        P("area", None, "tm"),
        P("area", None, "tm"),
        P("area", None, "tm"),
        P("area", None, None, "tm"),
        P("area", None, None),
        P("area", None, None, None),
        P("area", None),
        P("area", None),
        P(),
        P("area", None, None),
        P("area", None, None),
        P("area", None, None),
        P("area", None),
        P("area", None),
        P("area", None),
        P("area", None, "tm"),
    )
    out_specs = (
        P("area", None, "tm"),
        P("area", None, "tm"),
        P("area", None, None, "tm"),
        P("area", None, "tm"),
    )
    return jax.shard_map(local, mesh=mesh, in_specs=in_specs, out_specs=out_specs, check_vma=False)
```

```python
import functools
import math

import jax
import jax.numpy as jnp
from jax import lax
from jax.experimental import pallas as pl
from jax.experimental.pallas import tpu as pltpu
from jax.sharding import PartitionSpec as P

ITERS = 2


dispatch_step = 0.5


def padded_2(x, sides, width):
    for axis, dim in sides:
        size, length = (lax.axis_size(axis), x.shape[dim])
        up = [(i, (i + 1) % size) for i in range(size - 1)]
        down = [(j, i) for i, j in up]
        last = lax.slice_in_dim(x, length - width, length, axis=dim)
        leading = lax.slice_in_dim(x, 0, width, axis=dim)
        before = lax.ppermute(last, axis, up)
        after = lax.ppermute(leading, axis, down)
        x = jnp.concatenate([before, x, after], axis=dim)
    return x


def shifted_in(x, lane, step, fill):
    count = x.shape[1]
    ahead = pltpu.roll(x, step, 1)
    behind = pltpu.roll(x, count - step, 1)
    source = pltpu.roll(lane, step, 1)
    moved = jnp.where(source == lane - step, ahead, behind)
    return jnp.where(lane >= step, moved, fill)


def scan_kernel(kept_ref, balance_ref, gain_ref, total_ref, state_ref, ends_ref, *, scale):
    kept = kept_ref[...]
    state = -gain_ref[...] * balance_ref[...] / scale
    lane = lax.broadcasted_iota(jnp.int32, kept.shape, 1)
    step = 1
    while step < kept.shape[1]:
        state = kept * shifted_in(state, lane, step, 0.0) + state
        kept = kept * shifted_in(kept, lane, step, 1.0)
        step *= 2
    total_ref[...] = kept
    state_ref[...] = state
    row = lax.broadcasted_iota(jnp.int32, ends_ref.shape, 1)
    kept_end = jnp.broadcast_to(jnp.transpose(kept)[-1:, :][None], ends_ref.shape)
    state_end = jnp.broadcast_to(jnp.transpose(state)[-1:, :][None], ends_ref.shape)
    ends_ref[...] = jnp.where(row == 0, kept_end, jnp.where(row == 1, state_end, 0.0))


def window_scan(kept, balance, gain, scale, copies):
    shape = jax.ShapeDtypeStruct(kept.shape, jnp.float32)
    ends = jax.ShapeDtypeStruct((copies, 8, kept.shape[0]), jnp.float32)
    kernel = functools.partial(scan_kernel, scale=scale)
    return pl.pallas_call(kernel, out_shape=(shape, shape, ends))(kept, balance, gain)


def carried_state(kept_last, state_last, position):
    state_in = jnp.zeros_like(state_last[0])
    for window in range(state_last.shape[0]):
        folded = kept_last[window] * state_in + state_last[window]
        state_in = jnp.where(window < position, folded, state_in)
    return state_in


def local(
    angle_start,
    dispatch_start,
    demand,
    price_start,
    susceptance,
    tile_inverse,
    cost_slope,
    ramp_weight,
    partner,
    boundary,
    tie_susceptance,
    tie_penalty,
    store_bus,
    store_gain,
    store_output,
    retention,
):
    area_count = lax.axis_size("area")
    area_here = lax.axis_index("area")
    position = lax.axis_index("tm")
    partners = jnp.take(partner, area_here, axis=1, mode="clip")
    edge_rows = boundary[0]
    store_rows = store_bus[0]
    matrix = susceptance[0]
    inverses = tile_inverse[0]
    tile_count = inverses.shape[0]
    tile_width = inverses.shape[1]
    bus_count = matrix.shape[0]
    hour_count = retention.shape[2]
    year_hours = hour_count * lax.axis_size("tm")
    kept_local = retention[0]
    angle_now = angle_start[0].astype(jnp.float32)
    dispatch = dispatch_start[0].astype(jnp.float32)
    price_now = price_start[0].astype(jnp.float32)
    demand_local = demand[0].astype(jnp.float32)
    tie_gain = tie_susceptance[0][:, :, None]
    penalty = tie_penalty[0][:, :, None]
    slope = cost_slope[0][:, None]
    ramp_local = ramp_weight[0][:, None]
    gain_local = store_gain[0][:, None]
    output_local = store_output[0][:, None]
    injection = jnp.zeros((bus_count, hour_count), jnp.float32)
    charge_state = jnp.zeros_like(kept_local)
    rounds, lines = edge_rows.shape

    slot_ids = jnp.arange(area_count, dtype=jnp.int32)
    round_ids = jnp.arange(rounds, dtype=jnp.int32)
    round_of = jnp.sum(jnp.where(partners[:, None] == slot_ids[None, :], round_ids[:, None], 0), axis=0)

    def exchanged(parts, shapes):
        lanes = 128
        blocks = [part.reshape(rounds, -1, lanes) for part in parts]
        blocks = [jnp.pad(b, ((0, 0), (0, -b.shape[1] % 8), (0, 0))) for b in blocks]
        sent = jnp.take(jnp.concatenate(blocks, axis=1), round_of, axis=0, mode="clip")
        got = lax.all_to_all(sent, "area", split_axis=0, concat_axis=0, tiled=True)
        got = jnp.take(got, partners, axis=0, mode="clip").reshape(rounds, -1)
        found, at = [], 0
        for shape in shapes:
            width = math.prod(shape[1:])
            found.append(got[:, at : at + width].reshape(shape))
            at += width
        return found

    kept_total = None
    price_far = None
    penalty_far = None
    mismatch = None
    for iteration in range(ITERS):
        rounded = angle_now.astype(jnp.bfloat16)
        own_edge = lax.optimization_barrier(rounded[edge_rows].astype(jnp.float32))
        if iteration == 0:
            far_edge, price_far, penalty_far = exchanged(
                (own_edge, price_now, tie_penalty[0]),
                (own_edge.shape, price_now.shape, tie_penalty[0].shape),
            )
            penalty_far = penalty_far[:, :, None]
        else:
            (far_edge,) = exchanged((own_edge,), (own_edge.shape,))
            price_far = price_far - penalty_far * mismatch
        mismatch = own_edge - far_edge
        tie_flow = tie_gain * mismatch + 0.5 * (price_now - price_far)
        spread = jnp.zeros((bus_count, hour_count), jnp.float32).at[edge_rows].add(tie_flow)
        fixed_part = demand_local - dispatch - injection + spread
        balance = jnp.dot(matrix, rounded, preferred_element_type=jnp.float32) + fixed_part
        padded = padded_2(dispatch, (("tm", 1),), 1)
        bend = padded[:, :-2] - 2.0 * dispatch + padded[:, 2:]
        dispatch_next = dispatch + dispatch_step * (balance - slope * dispatch) + ramp_local * bend
        kept_total, local_state, copies = window_scan(
            kept_local, balance[store_rows], gain_local, math.sqrt(year_hours), lax.axis_size("tm")
        )
        ends = lax.all_to_all(copies, "tm", split_axis=0, concat_axis=0, tiled=True)
        state_in = carried_state(ends[:, 0], ends[:, 1], position)
        charge_state = local_state + kept_total * state_in[:, None]
        injection = (
            jnp.zeros((bus_count, hour_count), jnp.float32)
            .at[store_rows]
            .add(output_local * charge_state)
        )
        sweep_rows = balance.astype(jnp.bfloat16).reshape(tile_count, tile_width, hour_count)
        correction = jnp.einsum(
            "tij,tjh->tih", inverses, sweep_rows, preferred_element_type=jnp.float32
        )
        angle_now = angle_now - correction.reshape(bus_count, hour_count)
        price_now = price_now + penalty * mismatch
        dispatch = dispatch_next
    return (
        angle_now[None],
        dispatch.astype(jnp.bfloat16)[None],
        price_now[None],
        charge_state[None],
    )


def solution(mesh):
    in_specs = (
        P("area", None, "tm"),
        P("area", None, "tm"),
        P("area", None, "tm"),
        P("area", None, None, "tm"),
        P("area", None, None),
        P("area", None, None, None),
        P("area", None),
        P("area", None),
        P(),
        P("area", None, None),
        P("area", None, None),
        P("area", None, None),
        P("area", None),
        P("area", None),
        P("area", None),
        P("area", None, "tm"),
    )
    out_specs = (
        P("area", None, "tm"),
        P("area", None, "tm"),
        P("area", None, None, "tm"),
        P("area", None, "tm"),
    )
    return jax.shard_map(local, mesh=mesh, in_specs=in_specs, out_specs=out_specs, check_vma=False)
```
